128 devices in a mesh: req: 2 (over core), seq: 64 (over z, y, x).
Axes of the slice: x: 4, y: 4, z: 4, core: 2. Of those that a mesh axis runs over, the one named last changes fastest.
Arguments:
- tokens: bfloat16 [4, 128, 1536], P(None, ('req', 'seq')), may hold values from -6 to 6
- lengths: int32 [128], P('req'), may hold values from 1 to 16384, as said below
- k_cache: bfloat16 [128, 4096, 256], P('req', 'seq'), may hold values from -500 to 500
- v_cache: bfloat16 [128, 4096, 256], P('req', 'seq'), may hold values from -12 to 12
- attn_gain: bfloat16 [1536], replicated, may hold values from 0.5 to 1.5
- w_qkv: bfloat16 [1536, 2048], replicated, may hold values from -0.15625 to 0.15625
- sink: float32 [12], replicated, may hold values from -1 to 3
- w_out: bfloat16 [1536, 1536], replicated, may hold values from -0.15625 to 0.15625
- moe_gain: bfloat16 [1536], replicated, may hold values from 0.5 to 1.5
- router: bfloat16 [1536, 32], replicated, may hold values from -0.15625 to 0.15625
- w_gate: bfloat16 [1536, 24576], P(None, ('req', 'seq')), may hold values from -0.15625 to 0.15625
- w_up: bfloat16 [1536, 24576], P(None, ('req', 'seq')), may hold values from -0.15625 to 0.15625
- w_down: bfloat16 [24576, 1536], P(('req', 'seq')), may hold values from -0.21875 to 0.21875
- routes: int32 [128, 4, 4], replicated, may hold values from 0 to 31, all different within a row; in each aligned block of 4 rows (0 to 3, 4 to 7, ..., all dimensions but the last counted through in order) at most 2 rows name the same one
Outputs:
- outputs: bfloat16 [4, 128, 1536], P(None, ('req', 'seq'))
The draws below stay inside these ranges and needn't reach their ends.
Inputs may be any that keep to these rules, and one draw needn't show every extreme that they name: Each request has lengths positions before the first step; some request has all 16384 in every draw. `routes`: among the 4 tokens of one device's requests (requests 1 d .. 1 d + 1 - 1, all steps), no expert is named by more than 2 tokens, and in every draw some expert is named by exactly 2.
All inputs are finite; a program needn't handle non-finite values.
Results may differ from the reference program's by a relative error of at most 0.02.
Values may be sent and summed in bfloat16 or wider, within the bound.
No kernel may reach another device: no remote copies, remote signals or barrier semaphores. Data moves between devices by JAX's collectives and lax.ppermute only.
A program may use at most 512 MiB of HBM per device.

```python
import math
import jax
import jax.numpy as jnp
import numpy as np
from jax import lax

D = 1536
QH = 12
KVH = 2
HD = 128
E = 32
EFF = 768
TOP = 4
STEPS = 4
MOST = 2
ROWS_DEV = 1
CACHE = 4096
SPAN = 16384
B = 128
WINDOW = 4096


def draw_lengths(key, part):
    first, second, third = jax.random.split(jax.random.fold_in(key, 11), 3)
    left = jax.random.randint(first, (B,), 0, SPAN)
    right = jax.random.randint(second, (B,), 0, SPAN)
    spans = 1 + left * right // SPAN
    filled = jax.random.randint(third, (4,), 0, B)
    return spans.at[filled].set(SPAN).astype(jnp.int32)


def draw_k_cache(key, part):
    first = jax.random.fold_in(jax.random.fold_in(key, 23), 0)
    values = jnp.clip(2.0 * jax.random.normal(first, (B, CACHE, KVH * HD), jnp.float32), -12.0, 12.0)
    return values.astype(jnp.bfloat16)


def steps_of(rng, shape, cuts, low, top_value):
    level, own = 1.0, jax.random.fold_in(rng, 6)
    for dim, parts in cuts:
        draws = jnp.exp(jax.random.uniform(jax.random.fold_in(own, dim), (parts,), jnp.float32, low / len(cuts), top_value / len(cuts)))
        level = level * jnp.repeat(draws, shape[dim] // parts).reshape([-1 if axis == dim else 1 for axis in range(len(shape))])
    return level


def assign_block(stream_key, own, number, rows, count, top, bound, skew):
    order = jax.random.permutation(stream_key, count)
    packed, usual = portions_of(count, rows * top, bound, skew, True), portions_of(count, rows * top, bound, skew, False)
    places = jnp.arange(count)

    def named(sizes, turn):
        used = int((sizes > 0).sum())
        fixed = max(1, used // 4)
        passed = fixed + (places - fixed + turn * (used - fixed)) % max(1, count - fixed)
        return jnp.zeros((count,), jnp.int32).at[order[jnp.where(places < fixed, places, passed)]].set(jnp.asarray(sizes, jnp.int32))

    sizes = jnp.where(number % 4 == 0, named(packed, number // 4), named(usual, number - number // 4 - 1))
    mixed = jax.random.permutation(jax.random.fold_in(own, 3), count)
    source_of, taker = mixed[0:count // 2 * 2:2], mixed[1:count // 2 * 2:2]
    room = jnp.minimum(sizes[source_of] - 1, bound - sizes[taker]) // 2
    room = jnp.where((source_of == order[0]) | (taker == order[0]) | (sizes[taker] == 0), 0, jnp.maximum(room, 0))
    passed = jax.random.randint(jax.random.fold_in(own, 4), (count // 2,), 0, 1 << 20) % (room + 1)
    sizes = sizes.at[source_of].add(-passed).at[taker].add(passed)
    labels = jnp.searchsorted(jnp.cumsum(sizes), jnp.arange(rows * top), side="right").astype(jnp.int32)
    table = labels.reshape(top, rows).T
    table = table[jax.random.permutation(jax.random.fold_in(own, 1), rows)]
    turn = jax.random.randint(jax.random.fold_in(own, 2), (rows, 1), 0, top)
    return jnp.take_along_axis(table, (jnp.arange(top)[None, :] + turn) % top, axis=1)


def portions_of(count, total, reach, lean, full):
    loads = [(1 << 20) // math.isqrt(grade ** lean) + 1 for grade in range(1, count + 1)]
    largest = reach if full else min(reach, max(-(-total // count), total * loads[0] // sum(loads)))
    least = 1 if total - largest >= count - 1 else 0
    given, surplus = [largest] + [least] * (count - 1), total - largest - least * (count - 1)
    while surplus > 0:
        movable = [i for i in range(1, count) if given[i] < largest] or [i for i in range(1, count) if given[i] < reach]
        whole, left = sum([loads[i] for i in movable]), surplus
        for i in movable:
            more = min(reach - given[i], max(1, left * loads[i] // whole), surplus)
            given[i] = given[i] + more
            surplus = surplus - more
    return np.array(given)


def scatter_about(stream_key, extent, deviation, reach, cuts=(), kind=jnp.bfloat16):
    drawn = deviation * jax.random.normal(stream_key, extent, jnp.float32)
    if cuts:
        drawn = drawn * steps_of(stream_key, extent, cuts, -0.22, 0.18)
    return jnp.clip(drawn, -reach, reach).astype(kind)


def setup_inputs(seed: int = 0) -> dict:
    key_of = jax.random.split(jax.random.key(seed), 15)
    tokens = scatter_about(key_of[0], (STEPS, B, D), 1.0, 6.0, ((1, 128),))
    lengths = draw_lengths(jax.random.fold_in(key_of[14], 71), 0)
    k_cache = draw_k_cache(jax.random.fold_in(key_of[14], 71), 0)
    v_cache = scatter_about(key_of[3], (B, CACHE, KVH * HD), 2.0, 12.0, ((0, 2), (1, 64)))
    attn_gain = jnp.clip(1.0 + 0.1 * jax.random.normal(key_of[4], (D,), jnp.float32), 0.5, 1.5).astype(jnp.bfloat16)
    w_qkv = scatter_about(key_of[5], (D, (QH + 2 * KVH) * HD), D ** -0.5, 0.15625)
    sink = jnp.clip(jax.random.uniform(key_of[6], (QH,), jnp.float32, -1.0, 3.0), -1.0, 3.0)
    w_out = scatter_about(key_of[7], (QH * HD, D), (QH * HD) ** -0.5, 0.15625)
    moe_gain = jnp.clip(1.0 + 0.1 * jax.random.normal(key_of[8], (D,), jnp.float32), 0.5, 1.5).astype(jnp.bfloat16)
    router = scatter_about(key_of[9], (D, E), D ** -0.5, 0.15625)
    w_gate = scatter_about(key_of[10], (D, E * EFF), D ** -0.5, 0.15625, ((1, 128),))
    w_up = scatter_about(key_of[11], (D, E * EFF), D ** -0.5, 0.15625, ((1, 128),))
    w_down = scatter_about(key_of[12], (E * EFF, D), EFF ** -0.5, 0.21875, ((0, 128),))
    routes_keys = jax.random.split(jax.random.fold_in(key_of[13], 1), B * STEPS // (ROWS_DEV * STEPS))
    routes_turns = jax.random.permutation(jax.random.fold_in(key_of[13], 3), B * STEPS // (ROWS_DEV * STEPS))
    routes = jax.vmap(lambda own, number: assign_block(jax.random.fold_in(key_of[13], 2), own, number, ROWS_DEV * STEPS, E, TOP, MOST, 2))(routes_keys, routes_turns).reshape((B, STEPS, TOP))
    return dict(tokens=tokens, lengths=lengths, k_cache=k_cache, v_cache=v_cache, attn_gain=attn_gain, w_qkv=w_qkv, sink=sink, w_out=w_out, moe_gain=moe_gain, router=router, w_gate=w_gate, w_up=w_up, w_down=w_down, routes=routes)


def normalize(x, gain):
    xf = x.astype(jnp.float32)
    inv = lax.rsqrt(lax.optimization_barrier(jnp.mean(xf * xf, axis=-1, keepdims=True)) + 1e-05)
    return (xf * inv * gain.astype(jnp.float32)).astype(jnp.bfloat16)

def rotate(x, place):
    half = x.shape[-1] // 2
    index = jnp.arange(half, dtype=jnp.float32)
    inverse = jnp.exp(-jnp.log(1000000.0) * 2.0 * index / x.shape[-1])
    angle = place.astype(jnp.float32)[..., None, None] * inverse
    first = x[..., :half]
    second = x[..., half:]
    cosine = jnp.cos(angle)
    sine = jnp.sin(angle)
    return jnp.concatenate([first * cosine - second * sine, second * cosine + first * sine], axis=-1)

def reference(tokens, lengths, k_cache, v_cache, attn_gain, w_qkv, sink, w_out, moe_gain, router, w_gate, w_up, w_down, routes):
    heads_per = QH // KVH
    scale = HD ** (-0.5)
    block = 16
    tail_keys = jnp.zeros((B, STEPS, KVH, HD), jnp.bfloat16)
    tail_vals = jnp.zeros((B, STEPS, KVH, HD), jnp.bfloat16)
    gate_e = w_gate.reshape(D, E, EFF).transpose(1, 0, 2)
    up_e = w_up.reshape(D, E, EFF).transpose(1, 0, 2)
    down_e = w_down.reshape(E, EFF, D)
    sink_grid = sink.astype(jnp.float32).reshape(KVH, heads_per)
    results = []
    for step in range(STEPS):
        x = tokens[step]
        a = normalize(x, attn_gain)
        proj = jnp.dot(a, w_qkv, preferred_element_type=jnp.float32)
        place = lengths + step
        query = rotate(proj[:, :QH * HD].reshape(B, QH, HD), place).astype(jnp.bfloat16)
        fresh_key = rotate(proj[:, QH * HD:(QH + KVH) * HD].reshape(B, KVH, HD), place).astype(jnp.bfloat16)
        fresh_val = proj[:, (QH + KVH) * HD:].reshape(B, KVH, HD).astype(jnp.bfloat16)
        tail_keys = tail_keys.at[:, step].set(fresh_key)
        tail_vals = tail_vals.at[:, step].set(fresh_val)

        def attend(pieces):
            qb, kc, vc, lb, tk, tv = pieces
            count = qb.shape[0]
            qg = qb.astype(jnp.float32).reshape(count, KVH, heads_per, HD)
            kf = kc.astype(jnp.float32).reshape(count, CACHE, KVH, HD)
            vf = vc.astype(jnp.float32).reshape(count, CACHE, KVH, HD)
            scores = jnp.einsum('nkgd,nckd->nkgc', qg, kf) * scale
            key_slot = jnp.arange(CACHE, dtype=jnp.int32)
            back = jnp.mod(lb[:, None] - 1 - key_slot[None, :], WINDOW)
            valid = back < jnp.minimum(lb, WINDOW - 1 - step)[:, None]
            valid = valid[:, None, None, :]
            tail_scores = jnp.einsum('nkgd,nskd->nkgs', qg, tk.astype(jnp.float32)) * scale
            tail_valid = (jnp.arange(STEPS) <= step)[None, None, None, :]
            top = jnp.maximum(lax.optimization_barrier(jnp.max(jnp.where(valid, scores, -1e+30), axis=-1)), lax.optimization_barrier(jnp.max(jnp.where(tail_valid, tail_scores, -1e+30), axis=-1)))
            top = jnp.maximum(top, sink_grid[None])
            weights = jnp.where(valid, jnp.exp(scores - top[..., None]), 0.0)
            tail_w = jnp.where(tail_valid, jnp.exp(tail_scores - top[..., None]), 0.0)
            total = lax.optimization_barrier(jnp.sum(weights, axis=-1)) + lax.optimization_barrier(jnp.sum(tail_w, axis=-1)) + jnp.exp(sink_grid[None] - top)
            rounded = lax.optimization_barrier(weights.astype(jnp.bfloat16)).astype(jnp.float32)
            tail_rounded = lax.optimization_barrier(tail_w.astype(jnp.bfloat16)).astype(jnp.float32)
            mixed = jnp.einsum('nkgc,nckd->nkgd', rounded, vf) + jnp.einsum('nkgs,nskd->nkgd', tail_rounded, tv.astype(jnp.float32))
            return (mixed / total[..., None]).reshape(count, QH * HD).astype(jnp.bfloat16)
        shaped = (query.reshape(B // block, block, QH, HD), k_cache.reshape(B // block, block, CACHE, KVH * HD), v_cache.reshape(B // block, block, CACHE, KVH * HD), lengths.reshape(B // block, block), tail_keys.reshape(B // block, block, STEPS, KVH, HD), tail_vals.reshape(B // block, block, STEPS, KVH, HD))
        attn = lax.map(attend, shaped).reshape(B, QH * HD)
        h = (x.astype(jnp.float32) + jnp.dot(attn, w_out, preferred_element_type=jnp.float32)).astype(jnp.bfloat16)
        u = normalize(h, moe_gain)
        logits = jnp.dot(u, router, preferred_element_type=jnp.float32)
        picks = routes[:, step]
        chosen = jnp.take_along_axis(logits, picks, axis=1)
        share = jax.nn.softmax(chosen, axis=-1)
        dense = lax.optimization_barrier(jnp.sum(share[:, :, None] * (picks[:, :, None] == jnp.arange(E, dtype=jnp.int32)[None, None, :]).astype(jnp.float32), axis=1))

        def expert_step(total, pieces):
            gate_w, up_w, down_w, column = pieces
            hidden = (jax.nn.relu(jnp.dot(u, gate_w, preferred_element_type=jnp.float32)) * jnp.dot(u, up_w, preferred_element_type=jnp.float32)).astype(jnp.bfloat16)
            return (total + column[:, None] * jnp.dot(hidden, down_w, preferred_element_type=jnp.float32), None)
        moe, unused = lax.scan(expert_step, jnp.zeros((B, D), jnp.float32), (gate_e, up_e, down_e, dense.T))
        results.append((h.astype(jnp.float32) + moe).astype(jnp.bfloat16))
    return jnp.stack(results, axis=0)
```

```python
import jax
import jax.numpy as jnp
from jax import lax
from jax.sharding import PartitionSpec as P

D = 1536
QH = 12
KVH = 2
HD = 128
E = 32
EFF = 768
TOP = 4
STEPS = 4
MOST = 2


def normalize(x, gain):
    xf = x.astype(jnp.float32)
    inv = lax.rsqrt(jnp.mean(xf * xf, axis=-1, keepdims=True) + 1e-05)
    return (xf * inv * gain.astype(jnp.float32)).astype(jnp.bfloat16)


def rotate(x, place):
    half = x.shape[-1] // 2
    index = jnp.arange(half, dtype=jnp.float32)
    inverse = jnp.exp(-jnp.log(1000000.0) * 2.0 * index / x.shape[-1])
    angle = place.astype(jnp.float32)[..., None, None] * inverse
    first = x[..., :half]
    second = x[..., half:]
    cosine = jnp.cos(angle)
    sine = jnp.sin(angle)
    return jnp.concatenate(
        [first * cosine - second * sine, second * cosine + first * sine], axis=-1
    )


def on_device(
    tokens,
    lengths,
    k_cache,
    v_cache,
    attn_gain,
    w_qkv,
    sink,
    w_out,
    moe_gain,
    router,
    w_gate,
    w_up,
    w_down,
    routes,
):
    seq_count = lax.axis_size("seq")
    seq_place = lax.axis_index("seq")
    devices = lax.axis_size(("req", "seq"))
    device = lax.axis_index("req") * seq_count + seq_place
    group_rows = lengths.shape[0]
    local_pos = k_cache.shape[1]
    window = local_pos * seq_count
    heads_per = QH // KVH
    scale = HD ** (-0.5)
    heads_steps = STEPS * QH
    step_ids = jnp.arange(STEPS, dtype=jnp.int32)

    x = tokens[:, 0, :]
    own_len = lax.dynamic_index_in_dim(lengths, seq_place, 0, False)
    with jax.named_scope("qkv_projection"):
        a = normalize(x, attn_gain)
        proj = jnp.dot(a, w_qkv, preferred_element_type=jnp.float32)
        place = own_len + step_ids
        query = rotate(proj[:, : QH * HD].reshape(STEPS, QH, HD), place).astype(jnp.bfloat16)
        fresh_key = rotate(
            proj[:, QH * HD : (QH + KVH) * HD].reshape(STEPS, KVH, HD), place
        ).astype(jnp.bfloat16)
        fresh_val = proj[:, (QH + KVH) * HD :].reshape(STEPS, KVH, HD).astype(jnp.bfloat16)

    with jax.named_scope("query_exchange"):
        sent_q = jnp.broadcast_to(query.reshape(1, STEPS * QH * HD), (seq_count, STEPS * QH * HD))
        every_query = lax.all_to_all(sent_q, "seq", 0, 0, tiled=True)
    grouped_all = every_query.reshape(group_rows, STEPS, KVH, heads_per, HD)

    with jax.named_scope("slot_attention"):
        cache_keys = k_cache.reshape(group_rows, local_pos, KVH, HD)
        cache_vals = v_cache.reshape(group_rows, local_pos, KVH, HD)
        scores = (
            jnp.einsum("ntkgd,nckd->ntkgc", grouped_all, cache_keys, preferred_element_type=jnp.float32)
            * scale
        )
        key_slot = seq_place * local_pos + jnp.arange(local_pos, dtype=jnp.int32)
        back = jnp.mod(lengths[:, None, None] - 1 - key_slot[None, None, :], window)
        reach = jnp.minimum(lengths[:, None, None], window - 1 - step_ids[None, :, None])
        valid = (back < reach)[:, :, None, None, :]
        peak_local = jnp.max(jnp.where(valid, scores, -1e30), axis=-1)
        weights = jnp.where(valid, jnp.exp(scores - peak_local[..., None]), 0.0)
        total_local = jnp.sum(weights, axis=-1)
        mixed_local = jnp.einsum(
            "ntkgc,nckd->ntkgd",
            weights.astype(jnp.bfloat16),
            cache_vals,
            preferred_element_type=jnp.float32,
        )
        stats = jnp.concatenate(
            [
                total_local.reshape(group_rows, heads_steps),
                peak_local.reshape(group_rows, heads_steps),
                jnp.zeros((group_rows, HD - 2 * heads_steps), jnp.float32),
            ],
            axis=-1,
        )
        packed = jnp.concatenate(
            [mixed_local.reshape(group_rows, heads_steps, HD), stats[:, None, :]], axis=1
        )

    with jax.named_scope("partial_exchange"):
        parts = lax.all_to_all(packed, "seq", 0, 0, tiled=True)

    with jax.named_scope("merge_attention"):
        mixed_s = parts[:, :heads_steps, :].reshape(seq_count, STEPS, KVH, heads_per, HD)
        total_s = parts[:, heads_steps, :heads_steps].reshape(seq_count, STEPS, KVH, heads_per)
        peak_s = parts[:, heads_steps, heads_steps : 2 * heads_steps].reshape(
            seq_count, STEPS, KVH, heads_per
        )
        grouped = query.reshape(STEPS, KVH, heads_per, HD)
        tail_scores = (
            jnp.einsum("tkgd,skd->tkgs", grouped, fresh_key, preferred_element_type=jnp.float32)
            * scale
        )
        tail_valid = (step_ids[None, :] <= step_ids[:, None])[:, None, None, :]
        sink_grid = sink.reshape(KVH, heads_per)[None]
        final = jnp.maximum(
            jnp.maximum(jnp.max(peak_s, axis=0), jnp.max(jnp.where(tail_valid, tail_scores, -1e30), axis=-1)),
            sink_grid,
        )
        shift = jnp.exp(peak_s - final[None])
        tail_w = jnp.where(tail_valid, jnp.exp(tail_scores - final[..., None]), 0.0)
        denom = (
            jnp.sum(total_s * shift, axis=0)
            + jnp.sum(tail_w, axis=-1)
            + jnp.exp(sink_grid - final)
        )
        mixed = jnp.sum(mixed_s * shift[..., None], axis=0) + jnp.einsum(
            "tkgs,skd->tkgd",
            tail_w.astype(jnp.bfloat16),
            fresh_val,
            preferred_element_type=jnp.float32,
        )
        attn = (mixed / denom[..., None]).reshape(STEPS, QH * HD).astype(jnp.bfloat16)

    with jax.named_scope("attention_output"):
        h = (
            x.astype(jnp.float32) + jnp.dot(attn, w_out, preferred_element_type=jnp.float32)
        ).astype(jnp.bfloat16)
        u = normalize(h, moe_gain)

    with jax.named_scope("route"):
        picks = lax.dynamic_index_in_dim(routes, device, 0, False)
        experts = jnp.arange(E, dtype=jnp.int32)
        onehot = (picks[:, :, None] == experts[None, None, :]).astype(jnp.float32)
        logits = jnp.dot(u, router, preferred_element_type=jnp.float32)
        chosen = jnp.sum(onehot * logits[:, None, :], axis=-1)
        share = jax.nn.softmax(chosen, axis=-1)
        weight_te = jnp.sum(share[:, :, None] * onehot, axis=1)
        named = jnp.any(picks[:, :, None] == experts[None, None, :], axis=1)
        rank = jnp.cumsum(named.astype(jnp.int32), axis=0) - 1
        slots = jnp.arange(MOST, dtype=jnp.int32)
        select = (named[:, :, None] & (rank[:, :, None] == slots[None, None, :])).astype(jnp.float32)
        dispatch = jnp.einsum(
            "tej,tm->ejm", select.astype(jnp.bfloat16), u, preferred_element_type=jnp.float32
        ).astype(jnp.bfloat16)
        per_device = devices // E
        sent_u = jnp.broadcast_to(
            dispatch[:, None], (E, per_device, MOST, D)
        ).reshape(devices, MOST, D)

    with jax.named_scope("token_dispatch"):
        arrived = lax.all_to_all(sent_u, ("req", "seq"), 0, 0, tiled=True)

    with jax.named_scope("expert_quarter"):
        rows_in = arrived.reshape(devices * MOST, D)
        hidden = (
            jax.nn.relu(jnp.dot(rows_in, w_gate, preferred_element_type=jnp.float32))
            * jnp.dot(rows_in, w_up, preferred_element_type=jnp.float32)
        ).astype(jnp.bfloat16)
        produced = jnp.dot(hidden, w_down, preferred_element_type=jnp.float32).reshape(
            devices, MOST, D
        )

    with jax.named_scope("expert_return"):
        returned = lax.all_to_all(produced, ("req", "seq"), 0, 0, tiled=True)

    with jax.named_scope("expert_sum"):
        by_expert = jnp.sum(returned.reshape(E, per_device, MOST, D), axis=1)
        mix = (weight_te[:, :, None] * select).reshape(STEPS, E * MOST)
        moe = jnp.dot(
            mix, by_expert.reshape(E * MOST, D), precision=lax.Precision.HIGHEST,
            preferred_element_type=jnp.float32,
        )
        out = (h.astype(jnp.float32) + moe).astype(jnp.bfloat16)
    return out[:, None, :]


def solution(mesh):
    in_specs = (
        P(None, ("req", "seq"), None),
        P("req"),
        P("req", "seq", None),
        P("req", "seq", None),
        P(),
        P(),
        P(),
        P(),
        P(),
        P(),
        P(None, ("req", "seq")),
        P(None, ("req", "seq")),
        P(("req", "seq"), None),
        P(),
    )
    out_specs = P(None, ("req", "seq"), None)
    return jax.shard_map(
        on_device, mesh=mesh, in_specs=in_specs, out_specs=out_specs, check_vma=False
    )
```

```python
import jax
import jax.numpy as jnp
from jax import lax
from jax.sharding import PartitionSpec as P

D = 1536
QH = 12
KVH = 2
HD = 128
E = 32
EFF = 768
TOP = 4
STEPS = 4
MOST = 2


def normalize(x, gain):
    xf = x.astype(jnp.float32)
    inv = lax.rsqrt(jnp.mean(xf * xf, axis=-1, keepdims=True) + 1e-05)
    return (xf * inv * gain.astype(jnp.float32)).astype(jnp.bfloat16)


def rotate(x, place):
    half = x.shape[-1] // 2
    index = jnp.arange(half, dtype=jnp.float32)
    inverse = jnp.exp(-jnp.log(1000000.0) * 2.0 * index / x.shape[-1])
    angle = place.astype(jnp.float32)[..., None, None] * inverse
    first = x[..., :half]
    second = x[..., half:]
    cosine = jnp.cos(angle)
    sine = jnp.sin(angle)
    return jnp.concatenate(
        [first * cosine - second * sine, second * cosine + first * sine], axis=-1
    )


def on_device(
    tokens,
    lengths,
    k_cache,
    v_cache,
    attn_gain,
    w_qkv,
    sink,
    w_out,
    moe_gain,
    router,
    w_gate,
    w_up,
    w_down,
    routes,
):
    seq_count = lax.axis_size("seq")
    seq_place = lax.axis_index("seq")
    devices = lax.axis_size(("req", "seq"))
    device = lax.axis_index("req") * seq_count + seq_place
    group_rows = lengths.shape[0]
    local_pos = k_cache.shape[1]
    window = local_pos * seq_count
    heads_per = QH // KVH
    scale = HD ** (-0.5)
    step_ids = jnp.arange(STEPS, dtype=jnp.int32)

    x = tokens[:, 0, :]
    own_len = jnp.sum(jnp.where(jnp.arange(group_rows) == seq_place, lengths, 0))
    with jax.named_scope("qkv_projection"):
        a = normalize(x, attn_gain)
        proj = jnp.dot(a, w_qkv, preferred_element_type=jnp.float32)
        place = own_len + step_ids
        query = rotate(proj[:, : QH * HD].reshape(STEPS, QH, HD), place).astype(jnp.bfloat16)
        fresh_key = rotate(
            proj[:, QH * HD : (QH + KVH) * HD].reshape(STEPS, KVH, HD), place
        ).astype(jnp.bfloat16)
        fresh_val = proj[:, (QH + KVH) * HD :].reshape(STEPS, KVH, HD).astype(jnp.bfloat16)

    per_head = STEPS * heads_per
    rows_q = KVH * per_head
    q_heads = query.reshape(STEPS, KVH, heads_per, HD).transpose(1, 0, 2, 3)
    with jax.named_scope("query_exchange"):
        sent_q = jnp.broadcast_to(q_heads.reshape(1, rows_q, HD), (seq_count, rows_q, HD))
        every_query = lax.all_to_all(sent_q, "seq", 0, 0, tiled=True)

    with jax.named_scope("slot_attention"):
        key_slot = seq_place * local_pos + jnp.arange(local_pos, dtype=jnp.int32)
        back = jnp.mod(lengths[:, None] - 1 - key_slot[None, :], window)
        row_step = jnp.arange(per_head, dtype=jnp.int32) // heads_per
        reach = jnp.minimum(lengths[:, None], window - 1 - row_step[None, :])
        valid = back[:, None, :] < reach[:, :, None]
        mixed_heads, total_heads, hi_heads, mid_heads = [], [], [], []
        for k in range(KVH):
            q_k = every_query[:, k * per_head : (k + 1) * per_head, :]
            keys_k = k_cache[:, :, k * HD : (k + 1) * HD]
            vals_k = v_cache[:, :, k * HD : (k + 1) * HD]
            scores = (
                jnp.einsum("nrd,ncd->nrc", q_k, keys_k, preferred_element_type=jnp.float32)
                * scale
            )
            peak = jnp.max(jnp.where(valid, scores, -1e30), axis=-1)
            hi = peak.astype(jnp.bfloat16)
            mid = (peak - hi.astype(jnp.float32)).astype(jnp.bfloat16)
            shard_peak = hi.astype(jnp.float32) + mid.astype(jnp.float32)
            weights = jnp.where(valid, jnp.exp(scores - shard_peak[..., None]), 0.0)
            total_heads.append(jnp.sum(weights, axis=-1))
            mixed_heads.append(
                jnp.einsum(
                    "nrc,ncd->nrd",
                    weights.astype(jnp.bfloat16),
                    vals_k,
                    preferred_element_type=jnp.float32,
                )
            )
            hi_heads.append(hi)
            mid_heads.append(mid)
        stats = jnp.stack(
            [
                jnp.concatenate(total_heads, axis=1),
                jnp.concatenate(hi_heads, axis=1).astype(jnp.float32),
                jnp.concatenate(mid_heads, axis=1).astype(jnp.float32),
            ],
            axis=1,
        )
        stats = jnp.pad(stats, ((0, 0), (0, 16 - 3), (0, HD - rows_q)))
        packed = jnp.concatenate(mixed_heads + [stats], axis=1).astype(jnp.bfloat16)

    with jax.named_scope("partial_exchange"):
        parts = lax.all_to_all(packed, "seq", 0, 0, tiled=True)

    with jax.named_scope("merge_attention"):
        mixed_s = parts[:, :rows_q, :].astype(jnp.float32).reshape(
            seq_count, KVH, STEPS, heads_per, HD
        )
        total_s = parts[:, rows_q, :rows_q].astype(jnp.float32).reshape(
            seq_count, KVH, STEPS, heads_per
        )
        peak_s = (
            parts[:, rows_q + 1, :rows_q].astype(jnp.float32)
            + parts[:, rows_q + 2, :rows_q].astype(jnp.float32)
        ).reshape(seq_count, KVH, STEPS, heads_per)
        tail_scores = (
            jnp.einsum("ktgd,skd->ktgs", q_heads, fresh_key, preferred_element_type=jnp.float32)
            * scale
        )
        tail_valid = (step_ids[None, :] <= step_ids[:, None])[None, :, None, :]
        sink_grid = sink.reshape(KVH, 1, heads_per)
        final = jnp.maximum(
            jnp.maximum(jnp.max(peak_s, axis=0), jnp.max(jnp.where(tail_valid, tail_scores, -1e30), axis=-1)),
            sink_grid,
        )
        shift = jnp.exp(peak_s - final[None])
        tail_w = jnp.where(tail_valid, jnp.exp(tail_scores - final[..., None]), 0.0)
        denom = (
            jnp.sum(total_s * shift, axis=0)
            + jnp.sum(tail_w, axis=-1)
            + jnp.exp(sink_grid - final)
        )
        mixed = jnp.sum(mixed_s * shift[..., None], axis=0) + jnp.einsum(
            "ktgs,skd->ktgd",
            tail_w.astype(jnp.bfloat16),
            fresh_val,
            preferred_element_type=jnp.float32,
        )
        attn = (
            (mixed / denom[..., None]).transpose(1, 0, 2, 3).reshape(STEPS, QH * HD).astype(jnp.bfloat16)
        )

    with jax.named_scope("attention_output"):
        h = (
            x.astype(jnp.float32) + jnp.dot(attn, w_out, preferred_element_type=jnp.float32)
        ).astype(jnp.bfloat16)
        u = normalize(h, moe_gain)

    with jax.named_scope("route"):
        row_ids = jnp.arange(routes.shape[0], dtype=jnp.int32)
        picks = jnp.sum(jnp.where((row_ids == device)[:, None, None], routes, 0), axis=0)
        experts = jnp.arange(E, dtype=jnp.int32)
        onehot = (picks[:, :, None] == experts[None, None, :]).astype(jnp.float32)
        logits = jnp.dot(u, router, preferred_element_type=jnp.float32)
        chosen = jnp.sum(onehot * logits[:, None, :], axis=-1)
        share = jax.nn.softmax(chosen, axis=-1)
        weight_te = jnp.sum(share[:, :, None] * onehot, axis=1)
        named = jnp.any(picks[:, :, None] == experts[None, None, :], axis=1)
        rank = jnp.cumsum(named.astype(jnp.int32), axis=0) - 1
        slots = jnp.arange(MOST, dtype=jnp.int32)
        select = (named[:, :, None] & (rank[:, :, None] == slots[None, None, :])).astype(jnp.float32)
        dispatch = jnp.einsum(
            "tej,tm->ejm", select.astype(jnp.bfloat16), u, preferred_element_type=jnp.float32
        ).astype(jnp.bfloat16)
        per_device = devices // E
        sent_u = jnp.broadcast_to(
            dispatch[:, None], (E, per_device, MOST, D)
        ).reshape(devices, MOST, D)

    with jax.named_scope("token_dispatch"):
        arrived = lax.all_to_all(sent_u, ("req", "seq"), 0, 0, tiled=True)

    with jax.named_scope("expert_quarter"):
        rows_in = arrived.reshape(devices * MOST, D)
        hidden = (
            jax.nn.relu(jnp.dot(rows_in, w_gate, preferred_element_type=jnp.float32))
            * jnp.dot(rows_in, w_up, preferred_element_type=jnp.float32)
        ).astype(jnp.bfloat16)
        produced = (
            jnp.dot(hidden, w_down, preferred_element_type=jnp.float32)
            .astype(jnp.bfloat16)
            .reshape(devices, MOST, D)
        )

    with jax.named_scope("expert_return"):
        returned = lax.all_to_all(produced, ("req", "seq"), 0, 0, tiled=True)

    with jax.named_scope("expert_sum"):
        by_expert = jnp.sum(returned.astype(jnp.float32).reshape(E, per_device, MOST, D), axis=1)
        mix = (weight_te[:, :, None] * select).reshape(STEPS, E * MOST)
        moe = jnp.dot(
            mix, by_expert.reshape(E * MOST, D), precision=lax.Precision.HIGHEST,
            preferred_element_type=jnp.float32,
        )
        out = (h.astype(jnp.float32) + moe).astype(jnp.bfloat16)
    return out[:, None, :]


def solution(mesh):
    in_specs = (
        P(None, ("req", "seq"), None),
        P("req"),
        P("req", "seq", None),
        P("req", "seq", None),
        P(),
        P(),
        P(),
        P(),
        P(),
        P(),
        P(None, ("req", "seq")),
        P(None, ("req", "seq")),
        P(("req", "seq"), None),
        P(),
    )
    out_specs = P(None, ("req", "seq"), None)
    return jax.shard_map(
        on_device, mesh=mesh, in_specs=in_specs, out_specs=out_specs, check_vma=False
    )
```

```python
import jax
import jax.numpy as jnp
from jax import lax
from jax.sharding import PartitionSpec as P

D = 1536
QH = 12
KVH = 2
HD = 128
E = 32
EFF = 768
TOP = 4
STEPS = 4
MOST = 2


def normalize(x, gain):
    xf = x.astype(jnp.float32)
    inv = lax.rsqrt(jnp.mean(xf * xf, axis=-1, keepdims=True) + 1e-05)
    return (xf * inv * gain.astype(jnp.float32)).astype(jnp.bfloat16)


def rotate(x, place):
    half = x.shape[-1] // 2
    index = jnp.arange(half, dtype=jnp.float32)
    inverse = jnp.exp(-jnp.log(1000000.0) * 2.0 * index / x.shape[-1])
    angle = place.astype(jnp.float32)[..., None, None] * inverse
    first = x[..., :half]
    second = x[..., half:]
    cosine = jnp.cos(angle)
    sine = jnp.sin(angle)
    return jnp.concatenate(
        [first * cosine - second * sine, second * cosine + first * sine], axis=-1
    )


def on_device(
    tokens,
    lengths,
    k_cache,
    v_cache,
    attn_gain,
    w_qkv,
    sink,
    w_out,
    moe_gain,
    router,
    w_gate,
    w_up,
    w_down,
    routes,
):
    seq_count = lax.axis_size("seq")
    seq_place = lax.axis_index("seq")
    devices = lax.axis_size(("req", "seq"))
    device = lax.axis_index("req") * seq_count + seq_place
    group_rows = lengths.shape[0]
    local_pos = k_cache.shape[1]
    window = local_pos * seq_count
    heads_per = QH // KVH
    scale = HD ** (-0.5)
    step_ids = jnp.arange(STEPS, dtype=jnp.int32)

    x = tokens[:, 0, :]
    own_len = jnp.sum(jnp.where(jnp.arange(group_rows) == seq_place, lengths, 0))
    with jax.named_scope("qkv_projection"):
        a = normalize(x, attn_gain)
        proj = jnp.dot(a, w_qkv, preferred_element_type=jnp.float32)
        place = own_len + step_ids
        query = rotate(proj[:, : QH * HD].reshape(STEPS, QH, HD), place).astype(jnp.bfloat16)
    with jax.named_scope("fresh_key_value"):
        fresh_key = rotate(
            proj[:, QH * HD : (QH + KVH) * HD].reshape(STEPS, KVH, HD), place
        ).astype(jnp.bfloat16)
        fresh_val = proj[:, (QH + KVH) * HD :].reshape(STEPS, KVH, HD).astype(jnp.bfloat16)

    per_head = STEPS * heads_per
    rows_q = KVH * per_head
    q_heads = query.reshape(STEPS, KVH, heads_per, HD).transpose(1, 0, 2, 3)
    with jax.named_scope("query_exchange"):
        sent_q = jnp.broadcast_to(q_heads.reshape(1, rows_q, HD), (seq_count, rows_q, HD))
        every_query = lax.all_to_all(sent_q, "seq", 0, 0, tiled=True)

    with jax.named_scope("slot_attention"):
        key_slot = seq_place * local_pos + jnp.arange(local_pos, dtype=jnp.int32)
        back = jnp.mod(lengths[:, None] - 1 - key_slot[None, :], window)
        row_step = jnp.arange(per_head, dtype=jnp.int32) // heads_per
        reach = jnp.minimum(lengths[:, None], window - 1 - row_step[None, :])
        valid = back[:, None, :] < reach[:, :, None]
        mixed_heads, total_heads, hi_heads, mid_heads = [], [], [], []
        for k in range(KVH):
            q_k = every_query[:, k * per_head : (k + 1) * per_head, :]
            keys_k = k_cache[:, :, k * HD : (k + 1) * HD]
            vals_k = v_cache[:, :, k * HD : (k + 1) * HD]
            scores = (
                jnp.einsum("nrd,ncd->nrc", q_k, keys_k, preferred_element_type=jnp.float32)
                * scale
            )
            peak = jnp.max(jnp.where(valid, scores, -1e30), axis=-1)
            hi = peak.astype(jnp.bfloat16)
            mid = (peak - hi.astype(jnp.float32)).astype(jnp.bfloat16)
            shard_peak = hi.astype(jnp.float32) + mid.astype(jnp.float32)
            weights = jnp.where(valid, jnp.exp(scores - shard_peak[..., None]), 0.0)
            total_heads.append(jnp.sum(weights, axis=-1))
            mixed_heads.append(
                jnp.einsum(
                    "nrc,ncd->nrd",
                    weights.astype(jnp.bfloat16),
                    vals_k,
                    preferred_element_type=jnp.float32,
                )
            )
            hi_heads.append(hi)
            mid_heads.append(mid)
        stats = jnp.stack(
            [
                jnp.concatenate(total_heads, axis=1),
                jnp.concatenate(hi_heads, axis=1).astype(jnp.float32),
                jnp.concatenate(mid_heads, axis=1).astype(jnp.float32),
            ],
            axis=1,
        )
        stats = jnp.pad(stats, ((0, 0), (0, 8 - 3), (0, HD - rows_q)))
        packed = jnp.concatenate(mixed_heads + [stats], axis=1).astype(jnp.bfloat16)

    with jax.named_scope("partial_exchange"):
        parts = lax.all_to_all(packed, "seq", 0, 0, tiled=True)

    with jax.named_scope("merge_attention"):
        mixed_s = parts[:, :rows_q, :].astype(jnp.float32).reshape(
            seq_count, KVH, STEPS, heads_per, HD
        )
        total_s = parts[:, rows_q, :rows_q].astype(jnp.float32).reshape(
            seq_count, KVH, STEPS, heads_per
        )
        peak_s = (
            parts[:, rows_q + 1, :rows_q].astype(jnp.float32)
            + parts[:, rows_q + 2, :rows_q].astype(jnp.float32)
        ).reshape(seq_count, KVH, STEPS, heads_per)
        tail_scores = (
            jnp.einsum("ktgd,skd->ktgs", q_heads, fresh_key, preferred_element_type=jnp.float32)
            * scale
        )
        tail_valid = (step_ids[None, :] <= step_ids[:, None])[None, :, None, :]
        sink_grid = sink.reshape(KVH, 1, heads_per)
        final = jnp.maximum(
            jnp.maximum(jnp.max(peak_s, axis=0), jnp.max(jnp.where(tail_valid, tail_scores, -1e30), axis=-1)),
            sink_grid,
        )
        shift = jnp.exp(peak_s - final[None])
        tail_w = jnp.where(tail_valid, jnp.exp(tail_scores - final[..., None]), 0.0)
        denom = (
            jnp.sum(total_s * shift, axis=0)
            + jnp.sum(tail_w, axis=-1)
            + jnp.exp(sink_grid - final)
        )
        mixed = jnp.sum(mixed_s * shift[..., None], axis=0) + jnp.einsum(
            "ktgs,skd->ktgd",
            tail_w.astype(jnp.bfloat16),
            fresh_val,
            preferred_element_type=jnp.float32,
        )
        attn = (
            (mixed / denom[..., None]).transpose(1, 0, 2, 3).reshape(STEPS, QH * HD).astype(jnp.bfloat16)
        )

    with jax.named_scope("attention_output"):
        h = (
            x.astype(jnp.float32) + jnp.dot(attn, w_out, preferred_element_type=jnp.float32)
        ).astype(jnp.bfloat16)
        u = normalize(h, moe_gain)

    with jax.named_scope("route"):
        row_ids = jnp.arange(routes.shape[0], dtype=jnp.int32)
        picks = jnp.sum(jnp.where((row_ids == device)[:, None, None], routes, 0), axis=0)
        experts = jnp.arange(E, dtype=jnp.int32)
        onehot = (picks[:, :, None] == experts[None, None, :]).astype(jnp.float32)
        logits = jnp.dot(u, router, preferred_element_type=jnp.float32)
        chosen = jnp.sum(onehot * logits[:, None, :], axis=-1)
        share = jax.nn.softmax(chosen, axis=-1)
        weight_te = jnp.sum(share[:, :, None] * onehot, axis=1)
        named = jnp.any(picks[:, :, None] == experts[None, None, :], axis=1)
        rank = jnp.cumsum(named.astype(jnp.int32), axis=0) - 1
        slots = jnp.arange(MOST, dtype=jnp.int32)
        select = (named[:, :, None] & (rank[:, :, None] == slots[None, None, :])).astype(jnp.float32)
        dispatch = jnp.einsum(
            "tej,tm->ejm", select.astype(jnp.bfloat16), u, preferred_element_type=jnp.float32
        ).astype(jnp.bfloat16)
        per_device = devices // E
        sent_u = jnp.broadcast_to(
            dispatch[:, None], (E, per_device, MOST, D)
        ).reshape(devices, MOST, D)

    with jax.named_scope("token_dispatch"):
        arrived = lax.all_to_all(sent_u, ("req", "seq"), 0, 0, tiled=True)

    with jax.named_scope("expert_quarter"):
        hidden = (
            jax.nn.relu(jnp.einsum("sjm,mf->sjf", arrived, w_gate, preferred_element_type=jnp.float32))
            * jnp.einsum("sjm,mf->sjf", arrived, w_up, preferred_element_type=jnp.float32)
        ).astype(jnp.bfloat16)
        produced = jnp.einsum(
            "sjf,fm->sjm", hidden, w_down, preferred_element_type=jnp.float32
        ).astype(jnp.bfloat16)

    with jax.named_scope("expert_return"):
        returned = lax.all_to_all(produced, ("req", "seq"), 0, 0, tiled=True)

    with jax.named_scope("expert_sum"):
        by_expert = jnp.sum(returned.astype(jnp.float32).reshape(E, per_device, MOST, D), axis=1)
        mix = (weight_te[:, :, None] * select).reshape(STEPS, E * MOST)
        moe = jnp.dot(
            mix, by_expert.reshape(E * MOST, D), precision=lax.Precision.HIGHEST,
            preferred_element_type=jnp.float32,
        )
        out = (h.astype(jnp.float32) + moe).astype(jnp.bfloat16)
    return out[:, None, :]


def solution(mesh):
    in_specs = (
        P(None, ("req", "seq"), None),
        P("req"),
        P("req", "seq", None),
        P("req", "seq", None),
        P(),
        P(),
        P(),
        P(),
        P(),
        P(),
        P(None, ("req", "seq")),
        P(None, ("req", "seq")),
        P(("req", "seq"), None),
        P(),
    )
    out_specs = P(None, ("req", "seq"), None)
    return jax.shard_map(
        on_device, mesh=mesh, in_specs=in_specs, out_specs=out_specs, check_vma=False
    )
```

```python
import jax
import jax.numpy as jnp
from jax import lax
from jax.experimental import pallas as pl
from jax.experimental.pallas import tpu as pltpu
from jax.sharding import PartitionSpec as P

D = 1536
QH = 12
KVH = 2
HD = 128
E = 32
EFF = 768
TOP = 4
STEPS = 4
MOST = 2


def normalize(x, gain):
    xf = x.astype(jnp.float32)
    inv = lax.rsqrt(jnp.mean(xf * xf, axis=-1, keepdims=True) + 1e-05)
    return (xf * inv * gain.astype(jnp.float32)).astype(jnp.bfloat16)


def rotate(x, place):
    half = x.shape[-1] // 2
    index = jnp.arange(half, dtype=jnp.float32)
    inverse = jnp.exp(-jnp.log(1000000.0) * 2.0 * index / x.shape[-1])
    angle = place.astype(jnp.float32)[..., None, None] * inverse
    first = x[..., :half]
    second = x[..., half:]
    cosine = jnp.cos(angle)
    sine = jnp.sin(angle)
    return jnp.concatenate(
        [first * cosine - second * sine, second * cosine + first * sine], axis=-1
    )


def qkv_kernel(x_ref, gain_ref, w_ref, proj_ref):
    xf = x_ref[...].astype(jnp.float32)
    inv = lax.rsqrt(jnp.mean(xf * xf, axis=-1, keepdims=True) + 1e-05)
    a = (xf * inv * gain_ref[...].astype(jnp.float32)).astype(jnp.bfloat16)
    proj_ref[...] = jnp.dot(a, w_ref[...], preferred_element_type=jnp.float32)


def qkv_projection(x, gain, w_qkv):
    rows, width = x.shape
    columns = w_qkv.shape[1]
    return pl.pallas_call(
        qkv_kernel,
        out_shape=jax.ShapeDtypeStruct((rows, columns), jnp.float32),
        in_specs=[pl.BlockSpec(memory_space=pltpu.VMEM)] * 3,
        out_specs=pl.BlockSpec(memory_space=pltpu.VMEM),
        cost_estimate=pl.CostEstimate(
            flops=2 * rows * width * columns,
            transcendentals=rows,
            bytes_accessed=w_qkv.size * 2 + rows * (width * 2 + columns * 4),
        ),
    )(x, gain.reshape(1, width), w_qkv)


def output_projection_kernel(attn_ref, w_ref, x_ref, h_ref):
    product = jnp.dot(attn_ref[...], w_ref[...], preferred_element_type=jnp.float32)
    h_ref[...] = (x_ref[...].astype(jnp.float32) + product).astype(h_ref.dtype)


def output_projection(attn, w_out, x):
    rows, width = x.shape
    return pl.pallas_call(
        output_projection_kernel,
        out_shape=jax.ShapeDtypeStruct((rows, width), jnp.bfloat16),
        in_specs=[pl.BlockSpec(memory_space=pltpu.VMEM)] * 3,
        out_specs=pl.BlockSpec(memory_space=pltpu.VMEM),
        cost_estimate=pl.CostEstimate(
            flops=2 * rows * attn.shape[1] * width,
            transcendentals=0,
            bytes_accessed=w_out.size * 2 + 3 * rows * width * 2,
        ),
    )(attn, w_out, x)


def on_device(
    tokens,
    lengths,
    k_cache,
    v_cache,
    attn_gain,
    w_qkv,
    sink,
    w_out,
    moe_gain,
    router,
    w_gate,
    w_up,
    w_down,
    routes,
):
    seq_count = lax.axis_size("seq")
    seq_place = lax.axis_index("seq")
    devices = lax.axis_size(("req", "seq"))
    device = lax.axis_index("req") * seq_count + seq_place
    group_rows = lengths.shape[0]
    local_pos = k_cache.shape[1]
    window = local_pos * seq_count
    heads_per = QH // KVH
    scale = HD ** (-0.5)
    step_ids = jnp.arange(STEPS, dtype=jnp.int32)

    x = tokens[:, 0, :]
    own_len = jnp.sum(jnp.where(jnp.arange(group_rows) == seq_place, lengths, 0))
    with jax.named_scope("qkv_projection"):
        proj = qkv_projection(x, attn_gain, w_qkv)
        place = own_len + step_ids
        query = rotate(proj[:, : QH * HD].reshape(STEPS, QH, HD), place).astype(jnp.bfloat16)
    with jax.named_scope("fresh_key_value"):
        fresh_key = rotate(
            proj[:, QH * HD : (QH + KVH) * HD].reshape(STEPS, KVH, HD), place
        ).astype(jnp.bfloat16)
        fresh_val = proj[:, (QH + KVH) * HD :].reshape(STEPS, KVH, HD).astype(jnp.bfloat16)

    per_head = STEPS * heads_per
    rows_q = KVH * per_head
    q_heads = query.reshape(STEPS, KVH, heads_per, HD).transpose(1, 0, 2, 3)
    with jax.named_scope("query_exchange"):
        sent_q = jnp.broadcast_to(q_heads.reshape(1, rows_q, HD), (seq_count, rows_q, HD))
        every_query = lax.all_to_all(sent_q, "seq", 0, 0, tiled=True)

    with jax.named_scope("slot_attention"):
        key_slot = seq_place * local_pos + jnp.arange(local_pos, dtype=jnp.int32)
        back = jnp.mod(lengths[:, None] - 1 - key_slot[None, :], window)
        row_step = jnp.arange(per_head, dtype=jnp.int32) // heads_per
        reach = jnp.minimum(lengths[:, None], window - 1 - row_step[None, :])
        valid = back[:, None, :] < reach[:, :, None]
        mixed_heads, total_heads, hi_heads, mid_heads = [], [], [], []
        for k in range(KVH):
            q_k = every_query[:, k * per_head : (k + 1) * per_head, :]
            keys_k = k_cache[:, :, k * HD : (k + 1) * HD]
            vals_k = v_cache[:, :, k * HD : (k + 1) * HD]
            scores = (
                jnp.einsum("nrd,ncd->nrc", q_k, keys_k, preferred_element_type=jnp.float32)
                * scale
            )
            peak = jnp.max(jnp.where(valid, scores, -1e30), axis=-1)
            hi = peak.astype(jnp.bfloat16)
            mid = (peak - hi.astype(jnp.float32)).astype(jnp.bfloat16)
            shard_peak = hi.astype(jnp.float32) + mid.astype(jnp.float32)
            weights = jnp.where(valid, jnp.exp(scores - shard_peak[..., None]), 0.0)
            total_heads.append(jnp.sum(weights, axis=-1))
            mixed_heads.append(
                jnp.einsum(
                    "nrc,ncd->nrd",
                    weights.astype(jnp.bfloat16),
                    vals_k,
                    preferred_element_type=jnp.float32,
                )
            )
            hi_heads.append(hi)
            mid_heads.append(mid)
        stats = jnp.stack(
            [
                jnp.concatenate(total_heads, axis=1),
                jnp.concatenate(hi_heads, axis=1).astype(jnp.float32),
                jnp.concatenate(mid_heads, axis=1).astype(jnp.float32),
            ],
            axis=1,
        )
        stats = jnp.pad(stats, ((0, 0), (0, 8 - 3), (0, HD - rows_q)))
        packed = jnp.concatenate(mixed_heads + [stats], axis=1).astype(jnp.bfloat16)

    with jax.named_scope("partial_exchange"):
        parts = lax.all_to_all(packed, "seq", 0, 0, tiled=True)

    with jax.named_scope("merge_attention"):
        mixed_s = parts[:, :rows_q, :].astype(jnp.float32).reshape(
            seq_count, KVH, STEPS, heads_per, HD
        )
        total_s = parts[:, rows_q, :rows_q].astype(jnp.float32).reshape(
            seq_count, KVH, STEPS, heads_per
        )
        peak_s = (
            parts[:, rows_q + 1, :rows_q].astype(jnp.float32)
            + parts[:, rows_q + 2, :rows_q].astype(jnp.float32)
        ).reshape(seq_count, KVH, STEPS, heads_per)
        tail_scores = (
            jnp.einsum("ktgd,skd->ktgs", q_heads, fresh_key, preferred_element_type=jnp.float32)
            * scale
        )
        tail_valid = (step_ids[None, :] <= step_ids[:, None])[None, :, None, :]
        sink_grid = sink.reshape(KVH, 1, heads_per)
        final = jnp.maximum(
            jnp.maximum(jnp.max(peak_s, axis=0), jnp.max(jnp.where(tail_valid, tail_scores, -1e30), axis=-1)),
            sink_grid,
        )
        shift = jnp.exp(peak_s - final[None])
        tail_w = jnp.where(tail_valid, jnp.exp(tail_scores - final[..., None]), 0.0)
        denom = (
            jnp.sum(total_s * shift, axis=0)
            + jnp.sum(tail_w, axis=-1)
            + jnp.exp(sink_grid - final)
        )
        mixed = jnp.sum(mixed_s * shift[..., None], axis=0) + jnp.einsum(
            "ktgs,skd->ktgd",
            tail_w.astype(jnp.bfloat16),
            fresh_val,
            preferred_element_type=jnp.float32,
        )
        attn = (
            (mixed / denom[..., None]).transpose(1, 0, 2, 3).reshape(STEPS, QH * HD).astype(jnp.bfloat16)
        )

    with jax.named_scope("attention_output"):
        h = output_projection(attn, w_out, x)
        u = normalize(h, moe_gain)

    with jax.named_scope("route"):
        row_ids = jnp.arange(routes.shape[0], dtype=jnp.int32)
        picks = jnp.sum(jnp.where((row_ids == device)[:, None, None], routes, 0), axis=0)
        experts = jnp.arange(E, dtype=jnp.int32)
        onehot = (picks[:, :, None] == experts[None, None, :]).astype(jnp.float32)
        logits = jnp.dot(u, router, preferred_element_type=jnp.float32)
        chosen = jnp.sum(onehot * logits[:, None, :], axis=-1)
        share = jax.nn.softmax(chosen, axis=-1)
        weight_te = jnp.sum(share[:, :, None] * onehot, axis=1)
        named = jnp.any(picks[:, :, None] == experts[None, None, :], axis=1)
        rank = jnp.cumsum(named.astype(jnp.int32), axis=0) - 1
        slots = jnp.arange(MOST, dtype=jnp.int32)
        select = (named[:, :, None] & (rank[:, :, None] == slots[None, None, :])).astype(jnp.float32)
        dispatch = jnp.einsum(
            "tej,tm->ejm", select.astype(jnp.bfloat16), u, preferred_element_type=jnp.float32
        ).astype(jnp.bfloat16)
        per_device = devices // E
        sent_u = jnp.broadcast_to(
            dispatch[:, None], (E, per_device, MOST, D)
        ).reshape(devices, MOST, D)

    with jax.named_scope("token_dispatch"):
        arrived = lax.all_to_all(sent_u, ("req", "seq"), 0, 0, tiled=True)

    with jax.named_scope("expert_quarter"):
        rows_in = arrived.reshape(devices * MOST, D)
        hidden = (
            jax.nn.relu(jnp.dot(rows_in, w_gate, preferred_element_type=jnp.float32))
            * jnp.dot(rows_in, w_up, preferred_element_type=jnp.float32)
        ).astype(jnp.bfloat16)
        produced = (
            jnp.dot(hidden, w_down, preferred_element_type=jnp.float32)
            .astype(jnp.bfloat16)
            .reshape(devices, MOST, D)
        )

    with jax.named_scope("expert_return"):
        returned = lax.all_to_all(produced, ("req", "seq"), 0, 0, tiled=True)

    with jax.named_scope("expert_sum"):
        by_expert = jnp.sum(returned.astype(jnp.float32).reshape(E, per_device, MOST, D), axis=1)
        mix = (weight_te[:, :, None] * select).reshape(STEPS, E * MOST)
        moe = jnp.dot(
            mix, by_expert.reshape(E * MOST, D), precision=lax.Precision.HIGHEST,
            preferred_element_type=jnp.float32,
        )
        out = (h.astype(jnp.float32) + moe).astype(jnp.bfloat16)
    return out[:, None, :]


def solution(mesh):
    in_specs = (
        P(None, ("req", "seq"), None),
        P("req"),
        P("req", "seq", None),
        P("req", "seq", None),
        P(),
        P(),
        P(),
        P(),
        P(),
        P(),
        P(None, ("req", "seq")),
        P(None, ("req", "seq")),
        P(("req", "seq"), None),
        P(),
    )
    out_specs = P(None, ("req", "seq"), None)
    return jax.shard_map(
        on_device, mesh=mesh, in_specs=in_specs, out_specs=out_specs, check_vma=False
    )
```

```python
import jax
import jax.numpy as jnp
from jax import lax
from jax.sharding import PartitionSpec as P

D = 1536
QH = 12
KVH = 2
HD = 128
E = 32
EFF = 768
TOP = 4
STEPS = 4
MOST = 2


def normalize(x, gain):
    xf = x.astype(jnp.float32)
    inv = lax.rsqrt(jnp.mean(xf * xf, axis=-1, keepdims=True) + 1e-05)
    return (xf * inv * gain.astype(jnp.float32)).astype(jnp.bfloat16)


def rotate(x, place):
    half = x.shape[-1] // 2
    index = jnp.arange(half, dtype=jnp.float32)
    inverse = jnp.exp(-jnp.log(1000000.0) * 2.0 * index / x.shape[-1])
    angle = place.astype(jnp.float32)[..., None, None] * inverse
    first = x[..., :half]
    second = x[..., half:]
    cosine = jnp.cos(angle)
    sine = jnp.sin(angle)
    return jnp.concatenate(
        [first * cosine - second * sine, second * cosine + first * sine], axis=-1
    )


def on_device(
    tokens,
    lengths,
    k_cache,
    v_cache,
    attn_gain,
    w_qkv,
    sink,
    w_out,
    moe_gain,
    router,
    w_gate,
    w_up,
    w_down,
    routes,
):
    seq_count = lax.axis_size("seq")
    seq_place = lax.axis_index("seq")
    devices = lax.axis_size(("req", "seq"))
    device = lax.axis_index("req") * seq_count + seq_place
    group_rows = lengths.shape[0]
    local_pos = k_cache.shape[1]
    window = local_pos * seq_count
    heads_per = QH // KVH
    scale = HD ** (-0.5)
    step_ids = jnp.arange(STEPS, dtype=jnp.int32)

    x = tokens[:, 0, :]
    own_len = jnp.sum(jnp.where(jnp.arange(group_rows) == seq_place, lengths, 0))
    with jax.named_scope("qkv_projection"):
        a = normalize(x, attn_gain)
        proj = jnp.dot(a, w_qkv, preferred_element_type=jnp.float32)
        place = own_len + step_ids
        query = rotate(proj[:, : QH * HD].reshape(STEPS, QH, HD), place).astype(jnp.bfloat16)
    with jax.named_scope("fresh_key_value"):
        fresh_key = rotate(
            proj[:, QH * HD : (QH + KVH) * HD].reshape(STEPS, KVH, HD), place
        ).astype(jnp.bfloat16)
        fresh_val = proj[:, (QH + KVH) * HD :].reshape(STEPS, KVH, HD).astype(jnp.bfloat16)

    per_head = STEPS * heads_per
    rows_q = KVH * per_head
    q_heads = query.reshape(STEPS, KVH, heads_per, HD).transpose(1, 0, 2, 3)
    with jax.named_scope("query_exchange"):
        sent_q = jnp.broadcast_to(q_heads.reshape(1, rows_q, HD), (seq_count, rows_q, HD))
        every_query = lax.all_to_all(sent_q, "seq", 0, 0, tiled=True)

    with jax.named_scope("slot_attention"):
        key_slot = seq_place * local_pos + jnp.arange(local_pos, dtype=jnp.int32)
        back = jnp.mod(lengths[:, None] - 1 - key_slot[None, :], window)
        row_step = jnp.arange(per_head, dtype=jnp.int32) // heads_per
        reach = jnp.minimum(lengths[:, None], window - 1 - row_step[None, :])
        valid = back[:, None, :] < reach[:, :, None]
        mixed_heads, total_heads, hi_heads, mid_heads = [], [], [], []
        for k in range(KVH):
            q_k = every_query[:, k * per_head : (k + 1) * per_head, :]
            keys_k = k_cache[:, :, k * HD : (k + 1) * HD]
            vals_k = v_cache[:, :, k * HD : (k + 1) * HD]
            scores = (
                jnp.einsum("nrd,ncd->nrc", q_k, keys_k, preferred_element_type=jnp.float32)
                * scale
            )
            peak = jnp.max(jnp.where(valid, scores, -1e30), axis=-1)
            hi = peak.astype(jnp.bfloat16)
            mid = (peak - hi.astype(jnp.float32)).astype(jnp.bfloat16)
            shard_peak = hi.astype(jnp.float32) + mid.astype(jnp.float32)
            weights = jnp.where(valid, jnp.exp(scores - shard_peak[..., None]), 0.0)
            total_heads.append(jnp.sum(weights, axis=-1))
            mixed_heads.append(
                jnp.einsum(
                    "nrc,ncd->nrd",
                    weights.astype(jnp.bfloat16),
                    vals_k,
                    preferred_element_type=jnp.float32,
                )
            )
            hi_heads.append(hi)
            mid_heads.append(mid)
        stats = jnp.stack(
            [
                jnp.concatenate(total_heads, axis=1),
                jnp.concatenate(hi_heads, axis=1).astype(jnp.float32),
                jnp.concatenate(mid_heads, axis=1).astype(jnp.float32),
            ],
            axis=1,
        )
        stats = jnp.pad(stats, ((0, 0), (0, 8 - 3), (0, HD - rows_q)))
        packed = jnp.concatenate(mixed_heads + [stats], axis=1).astype(jnp.bfloat16)

    with jax.named_scope("partial_exchange"):
        parts = lax.all_to_all(packed, "seq", 0, 0, tiled=True)

    with jax.named_scope("merge_attention"):
        mixed_s = parts[:, :rows_q, :].astype(jnp.float32).reshape(
            seq_count, KVH, STEPS, heads_per, HD
        )
        total_s = parts[:, rows_q, :rows_q].astype(jnp.float32).reshape(
            seq_count, KVH, STEPS, heads_per
        )
        peak_s = (
            parts[:, rows_q + 1, :rows_q].astype(jnp.float32)
            + parts[:, rows_q + 2, :rows_q].astype(jnp.float32)
        ).reshape(seq_count, KVH, STEPS, heads_per)
        tail_scores = (
            jnp.einsum("ktgd,skd->ktgs", q_heads, fresh_key, preferred_element_type=jnp.float32)
            * scale
        )
        tail_valid = (step_ids[None, :] <= step_ids[:, None])[None, :, None, :]
        sink_grid = sink.reshape(KVH, 1, heads_per)
        final = jnp.maximum(
            jnp.maximum(jnp.max(peak_s, axis=0), jnp.max(jnp.where(tail_valid, tail_scores, -1e30), axis=-1)),
            sink_grid,
        )
        shift = jnp.exp(peak_s - final[None])
        tail_w = jnp.where(tail_valid, jnp.exp(tail_scores - final[..., None]), 0.0)
        denom = (
            jnp.sum(total_s * shift, axis=0)
            + jnp.sum(tail_w, axis=-1)
            + jnp.exp(sink_grid - final)
        )
        mixed = jnp.sum(mixed_s * shift[..., None], axis=0) + jnp.einsum(
            "ktgs,skd->ktgd",
            tail_w.astype(jnp.bfloat16),
            fresh_val,
            preferred_element_type=jnp.float32,
        )
        attn = (
            (mixed / denom[..., None]).transpose(1, 0, 2, 3).reshape(STEPS, QH * HD).astype(jnp.bfloat16)
        )

    with jax.named_scope("attention_output"):
        h = (
            x.astype(jnp.float32) + jnp.dot(attn, w_out, preferred_element_type=jnp.float32)
        ).astype(jnp.bfloat16)
        u = normalize(h, moe_gain)

    with jax.named_scope("route"):
        row_ids = jnp.arange(routes.shape[0], dtype=jnp.int32)
        picks = jnp.sum(jnp.where((row_ids == device)[:, None, None], routes, 0), axis=0)
        experts = jnp.arange(E, dtype=jnp.int32)
        onehot = (picks[:, :, None] == experts[None, None, :]).astype(jnp.float32)
        logits = jnp.dot(u, router, preferred_element_type=jnp.float32)
        chosen = jnp.sum(onehot * logits[:, None, :], axis=-1)
        share = jax.nn.softmax(chosen, axis=-1)
        weight_te = jnp.sum(share[:, :, None] * onehot, axis=1)
        named = jnp.any(picks[:, :, None] == experts[None, None, :], axis=1)
        rank = jnp.cumsum(named.astype(jnp.int32), axis=0) - 1
        slots = jnp.arange(MOST, dtype=jnp.int32)
        select = (named[:, :, None] & (rank[:, :, None] == slots[None, None, :])).astype(jnp.float32)
        dispatch = jnp.einsum(
            "tej,tm->ejm", select.astype(jnp.bfloat16), u, preferred_element_type=jnp.float32
        ).astype(jnp.bfloat16)
        per_device = devices // E
        sent_u = jnp.broadcast_to(
            dispatch[:, None], (E, per_device, MOST, D)
        ).reshape(devices, MOST, D)

    with jax.named_scope("token_dispatch"):
        arrived = lax.all_to_all(sent_u, ("req", "seq"), 0, 0, tiled=True)

    with jax.named_scope("expert_quarter"):
        rows_in = arrived.reshape(devices * MOST, D)
        hidden = (
            jax.nn.relu(jnp.dot(rows_in, w_gate, preferred_element_type=jnp.float32))
            * jnp.dot(rows_in, w_up, preferred_element_type=jnp.float32)
        ).astype(jnp.bfloat16)
        produced = (
            jnp.dot(hidden, w_down, preferred_element_type=jnp.float32)
            .astype(jnp.bfloat16)
            .reshape(devices, MOST, D)
        )

    with jax.named_scope("expert_return"):
        returned = lax.all_to_all(produced, ("req", "seq"), 0, 0, tiled=True)

    with jax.named_scope("expert_sum"):
        mix = jnp.broadcast_to(
            (weight_te[:, :, None] * select)[:, :, None, :], (STEPS, E, per_device, MOST)
        ).reshape(STEPS, devices * MOST)
        moe = jnp.dot(
            mix, returned.reshape(devices * MOST, D).astype(jnp.float32),
            precision=lax.Precision.HIGHEST, preferred_element_type=jnp.float32,
        )
        out = (h.astype(jnp.float32) + moe).astype(jnp.bfloat16)
    return out[:, None, :]


def solution(mesh):
    in_specs = (
        P(None, ("req", "seq"), None),
        P("req"),
        P("req", "seq", None),
        P("req", "seq", None),
        P(),
        P(),
        P(),
        P(),
        P(),
        P(),
        P(None, ("req", "seq")),
        P(None, ("req", "seq")),
        P(("req", "seq"), None),
        P(),
    )
    out_specs = P(None, ("req", "seq"), None)
    return jax.shard_map(
        on_device, mesh=mesh, in_specs=in_specs, out_specs=out_specs, check_vma=False
    )
```

```python
import jax
import jax.numpy as jnp
from jax import lax
from jax.sharding import PartitionSpec as P

D = 1536
QH = 12
KVH = 2
HD = 128
E = 32
EFF = 768
TOP = 4
STEPS = 4
MOST = 2


def normalize(x, gain):
    xf = x.astype(jnp.float32)
    inv = lax.rsqrt(jnp.mean(xf * xf, axis=-1, keepdims=True) + 1e-05)
    return (xf * inv * gain.astype(jnp.float32)).astype(jnp.bfloat16)


def rotate(x, place):
    half = x.shape[-1] // 2
    index = jnp.arange(half, dtype=jnp.float32)
    inverse = jnp.exp(-jnp.log(1000000.0) * 2.0 * index / x.shape[-1])
    angle = place.astype(jnp.float32)[..., None, None] * inverse
    first = x[..., :half]
    second = x[..., half:]
    cosine = jnp.cos(angle)
    sine = jnp.sin(angle)
    return jnp.concatenate(
        [first * cosine - second * sine, second * cosine + first * sine], axis=-1
    )


def on_device(
    tokens,
    lengths,
    k_cache,
    v_cache,
    attn_gain,
    w_qkv,
    sink,
    w_out,
    moe_gain,
    router,
    w_gate,
    w_up,
    w_down,
    routes,
):
    seq_count = lax.axis_size("seq")
    seq_place = lax.axis_index("seq")
    devices = lax.axis_size(("req", "seq"))
    device = lax.axis_index("req") * seq_count + seq_place
    group_rows = lengths.shape[0]
    local_pos = k_cache.shape[1]
    window = local_pos * seq_count
    heads_per = QH // KVH
    scale = HD ** (-0.5)
    step_ids = jnp.arange(STEPS, dtype=jnp.int32)

    x = tokens[:, 0, :]
    own_len = jnp.sum(jnp.where(jnp.arange(group_rows) == seq_place, lengths, 0))
    with jax.named_scope("qkv_projection"):
        a = normalize(x, attn_gain)
        proj = jnp.dot(a, w_qkv, preferred_element_type=jnp.float32)
        place = own_len + step_ids
        query = rotate(proj[:, : QH * HD].reshape(STEPS, QH, HD), place).astype(jnp.bfloat16)
    with jax.named_scope("fresh_key_value"):
        fresh_key = rotate(
            proj[:, QH * HD : (QH + KVH) * HD].reshape(STEPS, KVH, HD), place
        ).astype(jnp.bfloat16)
        fresh_val = proj[:, (QH + KVH) * HD :].reshape(STEPS, KVH, HD).astype(jnp.bfloat16)

    per_head = STEPS * heads_per
    rows_q = KVH * per_head
    q_heads = query.reshape(STEPS, KVH, heads_per, HD).transpose(1, 0, 2, 3)
    with jax.named_scope("query_exchange"):
        sent_q = jnp.broadcast_to(q_heads.reshape(1, rows_q, HD), (seq_count, rows_q, HD))
        every_query = lax.all_to_all(sent_q, "seq", 0, 0, tiled=True)

    with jax.named_scope("slot_attention"):
        key_slot = seq_place * local_pos + jnp.arange(local_pos, dtype=jnp.int32)
        back = jnp.mod(lengths[:, None] - 1 - key_slot[None, :], window)
        row_ids = jnp.arange(rows_q, dtype=jnp.int32)
        row_head = row_ids // per_head
        row_step = (row_ids % per_head) // heads_per
        reach = jnp.minimum(lengths[:, None], window - 1 - row_step[None, :])
        valid = back[:, None, :] < reach[:, :, None]
        lane_head = jnp.arange(KVH * HD, dtype=jnp.int32) // HD
        own_half = row_head[None, :, None] == lane_head[None, None, :]
        q_spread = jnp.where(
            own_half, jnp.concatenate([every_query] * KVH, axis=-1), jnp.zeros((), jnp.bfloat16)
        )
        scores = (
            jnp.einsum("nre,nce->nrc", q_spread, k_cache, preferred_element_type=jnp.float32)
            * scale
        )
        peak = jnp.max(jnp.where(valid, scores, -1e30), axis=-1)
        hi = peak.astype(jnp.bfloat16)
        mid = (peak - hi.astype(jnp.float32)).astype(jnp.bfloat16)
        shard_peak = hi.astype(jnp.float32) + mid.astype(jnp.float32)
        weights = jnp.where(valid, jnp.exp(scores - shard_peak[..., None]), 0.0)
        total = jnp.sum(weights, axis=-1)
        spread = jnp.einsum(
            "nrc,nce->nre", weights.astype(jnp.bfloat16), v_cache, preferred_element_type=jnp.float32
        )
        mixed_local = jnp.where(row_head[None, :, None] == 0, spread[..., :HD], spread[..., HD:])
        stats = jnp.stack(
            [total, hi.astype(jnp.float32), mid.astype(jnp.float32)], axis=1
        )
        stats = jnp.pad(stats, ((0, 0), (0, 8 - 3), (0, HD - rows_q)))
        packed = jnp.concatenate([mixed_local, stats], axis=1).astype(jnp.bfloat16)

    with jax.named_scope("partial_exchange"):
        parts = lax.all_to_all(packed, "seq", 0, 0, tiled=True)

    with jax.named_scope("merge_attention"):
        mixed_s = parts[:, :rows_q, :].astype(jnp.float32).reshape(
            seq_count, KVH, STEPS, heads_per, HD
        )
        total_s = parts[:, rows_q, :rows_q].astype(jnp.float32).reshape(
            seq_count, KVH, STEPS, heads_per
        )
        peak_s = (
            parts[:, rows_q + 1, :rows_q].astype(jnp.float32)
            + parts[:, rows_q + 2, :rows_q].astype(jnp.float32)
        ).reshape(seq_count, KVH, STEPS, heads_per)
        tail_scores = (
            jnp.einsum("ktgd,skd->ktgs", q_heads, fresh_key, preferred_element_type=jnp.float32)
            * scale
        )
        tail_valid = (step_ids[None, :] <= step_ids[:, None])[None, :, None, :]
        sink_grid = sink.reshape(KVH, 1, heads_per)
        final = jnp.maximum(
            jnp.maximum(jnp.max(peak_s, axis=0), jnp.max(jnp.where(tail_valid, tail_scores, -1e30), axis=-1)),
            sink_grid,
        )
        shift = jnp.exp(peak_s - final[None])
        tail_w = jnp.where(tail_valid, jnp.exp(tail_scores - final[..., None]), 0.0)
        denom = (
            jnp.sum(total_s * shift, axis=0)
            + jnp.sum(tail_w, axis=-1)
            + jnp.exp(sink_grid - final)
        )
        mixed = jnp.sum(mixed_s * shift[..., None], axis=0) + jnp.einsum(
            "ktgs,skd->ktgd",
            tail_w.astype(jnp.bfloat16),
            fresh_val,
            preferred_element_type=jnp.float32,
        )
        attn = (
            (mixed / denom[..., None]).transpose(1, 0, 2, 3).reshape(STEPS, QH * HD).astype(jnp.bfloat16)
        )

    with jax.named_scope("attention_output"):
        h = (
            x.astype(jnp.float32) + jnp.dot(attn, w_out, preferred_element_type=jnp.float32)
        ).astype(jnp.bfloat16)
        u = normalize(h, moe_gain)

    with jax.named_scope("route"):
        row_ids = jnp.arange(routes.shape[0], dtype=jnp.int32)
        picks = jnp.sum(jnp.where((row_ids == device)[:, None, None], routes, 0), axis=0)
        experts = jnp.arange(E, dtype=jnp.int32)
        onehot = (picks[:, :, None] == experts[None, None, :]).astype(jnp.float32)
        logits = jnp.dot(u, router, preferred_element_type=jnp.float32)
        chosen = jnp.sum(onehot * logits[:, None, :], axis=-1)
        share = jax.nn.softmax(chosen, axis=-1)
        weight_te = jnp.sum(share[:, :, None] * onehot, axis=1)
        named = jnp.any(picks[:, :, None] == experts[None, None, :], axis=1)
        rank = jnp.cumsum(named.astype(jnp.int32), axis=0) - 1
        slots = jnp.arange(MOST, dtype=jnp.int32)
        select = (named[:, :, None] & (rank[:, :, None] == slots[None, None, :])).astype(jnp.float32)
        dispatch = jnp.einsum(
            "tej,tm->ejm", select.astype(jnp.bfloat16), u, preferred_element_type=jnp.float32
        ).astype(jnp.bfloat16)
        per_device = devices // E
        sent_u = jnp.broadcast_to(
            dispatch[:, None], (E, per_device, MOST, D)
        ).reshape(devices, MOST, D)

    with jax.named_scope("token_dispatch"):
        arrived = lax.all_to_all(sent_u, ("req", "seq"), 0, 0, tiled=True)

    with jax.named_scope("expert_quarter"):
        hidden = (
            jax.nn.relu(jnp.einsum("sjm,mf->sjf", arrived, w_gate, preferred_element_type=jnp.float32))
            * jnp.einsum("sjm,mf->sjf", arrived, w_up, preferred_element_type=jnp.float32)
        ).astype(jnp.bfloat16)
        produced = jnp.einsum(
            "sjf,fm->sjm", hidden, w_down, preferred_element_type=jnp.float32
        ).astype(jnp.bfloat16)

    with jax.named_scope("expert_return"):
        returned = lax.all_to_all(produced, ("req", "seq"), 0, 0, tiled=True)

    with jax.named_scope("expert_sum"):
        by_expert = jnp.sum(returned.astype(jnp.float32).reshape(E, per_device, MOST, D), axis=1)
        mix = (weight_te[:, :, None] * select).reshape(STEPS, E * MOST)
        moe = jnp.dot(
            mix, by_expert.reshape(E * MOST, D), precision=lax.Precision.HIGHEST,
            preferred_element_type=jnp.float32,
        )
        out = (h.astype(jnp.float32) + moe).astype(jnp.bfloat16)
    return out[:, None, :]


def solution(mesh):
    in_specs = (
        P(None, ("req", "seq"), None),
        P("req"),
        P("req", "seq", None),
        P("req", "seq", None),
        P(),
        P(),
        P(),
        P(),
        P(),
        P(),
        P(None, ("req", "seq")),
        P(None, ("req", "seq")),
        P(("req", "seq"), None),
        P(),
    )
    out_specs = P(None, ("req", "seq"), None)
    return jax.shard_map(
        on_device, mesh=mesh, in_specs=in_specs, out_specs=out_specs, check_vma=False
    )
```

```python
import jax
import jax.numpy as jnp
from jax import lax
from jax.sharding import PartitionSpec as P

D = 1536
QH = 12
KVH = 2
HD = 128
E = 32
EFF = 768
TOP = 4
STEPS = 4
MOST = 2


def normalize(x, gain):
    xf = x.astype(jnp.float32)
    inv = lax.rsqrt(jnp.mean(xf * xf, axis=-1, keepdims=True) + 1e-05)
    return (xf * inv * gain.astype(jnp.float32)).astype(jnp.bfloat16)


def rotate(x, place):
    half = x.shape[-1] // 2
    index = jnp.arange(half, dtype=jnp.float32)
    inverse = jnp.exp(-jnp.log(1000000.0) * 2.0 * index / x.shape[-1])
    angle = place.astype(jnp.float32)[..., None, None] * inverse
    first = x[..., :half]
    second = x[..., half:]
    cosine = jnp.cos(angle)
    sine = jnp.sin(angle)
    return jnp.concatenate(
        [first * cosine - second * sine, second * cosine + first * sine], axis=-1
    )


def on_device(
    tokens,
    lengths,
    k_cache,
    v_cache,
    attn_gain,
    w_qkv,
    sink,
    w_out,
    moe_gain,
    router,
    w_gate,
    w_up,
    w_down,
    routes,
):
    seq_count = lax.axis_size("seq")
    seq_place = lax.axis_index("seq")
    devices = lax.axis_size(("req", "seq"))
    device = lax.axis_index("req") * seq_count + seq_place
    group_rows = lengths.shape[0]
    local_pos = k_cache.shape[1]
    window = local_pos * seq_count
    heads_per = QH // KVH
    scale = HD ** (-0.5)
    step_ids = jnp.arange(STEPS, dtype=jnp.int32)

    x = tokens[:, 0, :]
    per_head = STEPS * heads_per
    rows_q = KVH * per_head
    with jax.named_scope("token_exchange"):
        sent_x = jnp.broadcast_to(x[None], (seq_count, STEPS, D))
        every_x = lax.all_to_all(sent_x, "seq", 0, 0, tiled=True)

    with jax.named_scope("qkv_projection"):
        a_all = normalize(every_x.reshape(group_rows * STEPS, D), attn_gain)
        proj_all = jnp.dot(a_all, w_qkv, preferred_element_type=jnp.float32).reshape(
            group_rows, STEPS, (QH + 2 * KVH) * HD
        )
        place_all = lengths[:, None] + step_ids[None, :]
        query_all = rotate(proj_all[..., : QH * HD].reshape(group_rows, STEPS, QH, HD), place_all).astype(
            jnp.bfloat16
        )
        every_query = (
            query_all.reshape(group_rows, STEPS, KVH, heads_per, HD)
            .transpose(0, 2, 1, 3, 4)
            .reshape(group_rows, rows_q, HD)
        )

    with jax.named_scope("fresh_key_value"):
        mine = (jnp.arange(group_rows) == seq_place)[:, None, None]
        own_proj = jnp.sum(jnp.where(mine, proj_all[..., QH * HD :], 0.0), axis=0)
        own_len = jnp.sum(jnp.where(jnp.arange(group_rows) == seq_place, lengths, 0))
        place = own_len + step_ids
        fresh_key = rotate(own_proj[:, : KVH * HD].reshape(STEPS, KVH, HD), place).astype(jnp.bfloat16)
        fresh_val = own_proj[:, KVH * HD :].reshape(STEPS, KVH, HD).astype(jnp.bfloat16)
        q_heads = jnp.sum(
            jnp.where(mine, every_query.astype(jnp.float32), 0.0), axis=0
        ).astype(jnp.bfloat16).reshape(KVH, STEPS, heads_per, HD)

    with jax.named_scope("slot_attention"):
        key_slot = seq_place * local_pos + jnp.arange(local_pos, dtype=jnp.int32)
        back = jnp.mod(lengths[:, None] - 1 - key_slot[None, :], window)
        row_step = jnp.arange(per_head, dtype=jnp.int32) // heads_per
        reach = jnp.minimum(lengths[:, None], window - 1 - row_step[None, :])
        valid = back[:, None, :] < reach[:, :, None]
        mixed_heads, total_heads, hi_heads, mid_heads = [], [], [], []
        for k in range(KVH):
            q_k = every_query[:, k * per_head : (k + 1) * per_head, :]
            keys_k = k_cache[:, :, k * HD : (k + 1) * HD]
            vals_k = v_cache[:, :, k * HD : (k + 1) * HD]
            scores = (
                jnp.einsum("nrd,ncd->nrc", q_k, keys_k, preferred_element_type=jnp.float32)
                * scale
            )
            peak = jnp.max(jnp.where(valid, scores, -1e30), axis=-1)
            hi = peak.astype(jnp.bfloat16)
            mid = (peak - hi.astype(jnp.float32)).astype(jnp.bfloat16)
            shard_peak = hi.astype(jnp.float32) + mid.astype(jnp.float32)
            weights = jnp.where(valid, jnp.exp(scores - shard_peak[..., None]), 0.0)
            total_heads.append(jnp.sum(weights, axis=-1))
            mixed_heads.append(
                jnp.einsum(
                    "nrc,ncd->nrd",
                    weights.astype(jnp.bfloat16),
                    vals_k,
                    preferred_element_type=jnp.float32,
                )
            )
            hi_heads.append(hi)
            mid_heads.append(mid)
        stats = jnp.stack(
            [
                jnp.concatenate(total_heads, axis=1),
                jnp.concatenate(hi_heads, axis=1).astype(jnp.float32),
                jnp.concatenate(mid_heads, axis=1).astype(jnp.float32),
            ],
            axis=1,
        )
        stats = jnp.pad(stats, ((0, 0), (0, 8 - 3), (0, HD - rows_q)))
        packed = jnp.concatenate(mixed_heads + [stats], axis=1).astype(jnp.bfloat16)

    with jax.named_scope("partial_exchange"):
        parts = lax.all_to_all(packed, "seq", 0, 0, tiled=True)

    with jax.named_scope("merge_attention"):
        mixed_s = parts[:, :rows_q, :].astype(jnp.float32).reshape(
            seq_count, KVH, STEPS, heads_per, HD
        )
        total_s = parts[:, rows_q, :rows_q].astype(jnp.float32).reshape(
            seq_count, KVH, STEPS, heads_per
        )
        peak_s = (
            parts[:, rows_q + 1, :rows_q].astype(jnp.float32)
            + parts[:, rows_q + 2, :rows_q].astype(jnp.float32)
        ).reshape(seq_count, KVH, STEPS, heads_per)
        tail_scores = (
            jnp.einsum("ktgd,skd->ktgs", q_heads, fresh_key, preferred_element_type=jnp.float32)
            * scale
        )
        tail_valid = (step_ids[None, :] <= step_ids[:, None])[None, :, None, :]
        sink_grid = sink.reshape(KVH, 1, heads_per)
        final = jnp.maximum(
            jnp.maximum(jnp.max(peak_s, axis=0), jnp.max(jnp.where(tail_valid, tail_scores, -1e30), axis=-1)),
            sink_grid,
        )
        shift = jnp.exp(peak_s - final[None])
        tail_w = jnp.where(tail_valid, jnp.exp(tail_scores - final[..., None]), 0.0)
        denom = (
            jnp.sum(total_s * shift, axis=0)
            + jnp.sum(tail_w, axis=-1)
            + jnp.exp(sink_grid - final)
        )
        mixed = jnp.sum(mixed_s * shift[..., None], axis=0) + jnp.einsum(
            "ktgs,skd->ktgd",
            tail_w.astype(jnp.bfloat16),
            fresh_val,
            preferred_element_type=jnp.float32,
        )
        attn = (
            (mixed / denom[..., None]).transpose(1, 0, 2, 3).reshape(STEPS, QH * HD).astype(jnp.bfloat16)
        )

    with jax.named_scope("attention_output"):
        h = (
            x.astype(jnp.float32) + jnp.dot(attn, w_out, preferred_element_type=jnp.float32)
        ).astype(jnp.bfloat16)
        u = normalize(h, moe_gain)

    with jax.named_scope("route"):
        row_ids = jnp.arange(routes.shape[0], dtype=jnp.int32)
        picks = jnp.sum(jnp.where((row_ids == device)[:, None, None], routes, 0), axis=0)
        experts = jnp.arange(E, dtype=jnp.int32)
        onehot = (picks[:, :, None] == experts[None, None, :]).astype(jnp.float32)
        logits = jnp.dot(u, router, preferred_element_type=jnp.float32)
        chosen = jnp.sum(onehot * logits[:, None, :], axis=-1)
        share = jax.nn.softmax(chosen, axis=-1)
        weight_te = jnp.sum(share[:, :, None] * onehot, axis=1)
        named = jnp.any(picks[:, :, None] == experts[None, None, :], axis=1)
        rank = jnp.cumsum(named.astype(jnp.int32), axis=0) - 1
        slots = jnp.arange(MOST, dtype=jnp.int32)
        select = (named[:, :, None] & (rank[:, :, None] == slots[None, None, :])).astype(jnp.float32)
        dispatch = jnp.einsum(
            "tej,tm->ejm", select.astype(jnp.bfloat16), u, preferred_element_type=jnp.float32
        ).astype(jnp.bfloat16)
        per_device = devices // E
        sent_u = jnp.broadcast_to(
            dispatch[:, None], (E, per_device, MOST, D)
        ).reshape(devices, MOST, D)

    with jax.named_scope("token_dispatch"):
        arrived = lax.all_to_all(sent_u, ("req", "seq"), 0, 0, tiled=True)

    with jax.named_scope("expert_quarter"):
        rows_in = arrived.reshape(devices * MOST, D)
        hidden = (
            jax.nn.relu(jnp.dot(rows_in, w_gate, preferred_element_type=jnp.float32))
            * jnp.dot(rows_in, w_up, preferred_element_type=jnp.float32)
        ).astype(jnp.bfloat16)
        produced = (
            jnp.dot(hidden, w_down, preferred_element_type=jnp.float32)
            .astype(jnp.bfloat16)
            .reshape(devices, MOST, D)
        )

    with jax.named_scope("expert_return"):
        returned = lax.all_to_all(produced, ("req", "seq"), 0, 0, tiled=True)

    with jax.named_scope("expert_sum"):
        by_expert = jnp.sum(returned.astype(jnp.float32).reshape(E, per_device, MOST, D), axis=1)
        mix = (weight_te[:, :, None] * select).reshape(STEPS, E * MOST)
        moe = jnp.dot(
            mix, by_expert.reshape(E * MOST, D), precision=lax.Precision.HIGHEST,
            preferred_element_type=jnp.float32,
        )
        out = (h.astype(jnp.float32) + moe).astype(jnp.bfloat16)
    return out[:, None, :]


def solution(mesh):
    in_specs = (
        P(None, ("req", "seq"), None),
        P("req"),
        P("req", "seq", None),
        P("req", "seq", None),
        P(),
        P(),
        P(),
        P(),
        P(),
        P(),
        P(None, ("req", "seq")),
        P(None, ("req", "seq")),
        P(("req", "seq"), None),
        P(),
    )
    out_specs = P(None, ("req", "seq"), None)
    return jax.shard_map(
        on_device, mesh=mesh, in_specs=in_specs, out_specs=out_specs, check_vma=False
    )
```

```python
import jax
import jax.numpy as jnp
from jax import lax
from jax.sharding import PartitionSpec as P

D = 1536
QH = 12
KVH = 2
HD = 128
E = 32
EFF = 768
TOP = 4
STEPS = 4
MOST = 2


def normalize(x, gain):
    xf = x.astype(jnp.float32)
    inv = lax.rsqrt(jnp.mean(xf * xf, axis=-1, keepdims=True) + 1e-05)
    return (xf * inv * gain.astype(jnp.float32)).astype(jnp.bfloat16)


def rotate(x, place):
    half = x.shape[-1] // 2
    index = jnp.arange(half, dtype=jnp.float32)
    inverse = jnp.exp(-jnp.log(1000000.0) * 2.0 * index / x.shape[-1])
    angle = place.astype(jnp.float32)[..., None, None] * inverse
    first = x[..., :half]
    second = x[..., half:]
    cosine = jnp.cos(angle)
    sine = jnp.sin(angle)
    return jnp.concatenate(
        [first * cosine - second * sine, second * cosine + first * sine], axis=-1
    )


def on_device(
    tokens,
    lengths,
    k_cache,
    v_cache,
    attn_gain,
    w_qkv,
    sink,
    w_out,
    moe_gain,
    router,
    w_gate,
    w_up,
    w_down,
    routes,
):
    seq_count = lax.axis_size("seq")
    seq_place = lax.axis_index("seq")
    devices = lax.axis_size(("req", "seq"))
    device = lax.axis_index("req") * seq_count + seq_place
    group_rows = lengths.shape[0]
    local_pos = k_cache.shape[1]
    window = local_pos * seq_count
    heads_per = QH // KVH
    scale = HD ** (-0.5)
    step_ids = jnp.arange(STEPS, dtype=jnp.int32)

    x = tokens[:, 0, :]
    own_len = jnp.sum(jnp.where(jnp.arange(group_rows) == seq_place, lengths, 0))
    with jax.named_scope("qkv_projection"):
        a = normalize(x, attn_gain)
        proj = jnp.dot(a, w_qkv, preferred_element_type=jnp.float32)
        place = own_len + step_ids
        query = rotate(proj[:, : QH * HD].reshape(STEPS, QH, HD), place).astype(jnp.bfloat16)
    with jax.named_scope("fresh_key_value"):
        fresh_key = rotate(
            proj[:, QH * HD : (QH + KVH) * HD].reshape(STEPS, KVH, HD), place
        ).astype(jnp.bfloat16)
        fresh_val = proj[:, (QH + KVH) * HD :].reshape(STEPS, KVH, HD).astype(jnp.bfloat16)

    per_head = STEPS * heads_per
    rows_q = KVH * per_head
    q_heads = query.reshape(STEPS, KVH, heads_per, HD).transpose(1, 0, 2, 3)
    with jax.named_scope("query_exchange"):
        sent_q = jnp.broadcast_to(q_heads.reshape(1, rows_q, HD), (seq_count, rows_q, HD))
        every_query = lax.all_to_all(sent_q, "seq", 0, 0, tiled=True)

    with jax.named_scope("slot_attention"):
        key_slot = seq_place * local_pos + jnp.arange(local_pos, dtype=jnp.int32)
        back = jnp.mod(lengths[:, None] - 1 - key_slot[None, :], window)
        row_step = jnp.arange(per_head, dtype=jnp.int32) // heads_per
        reach = jnp.minimum(lengths[:, None], window - 1 - row_step[None, :])
        valid = back[:, None, :] < reach[:, :, None]
        mixed_heads, total_heads, hi_heads, mid_heads = [], [], [], []
        for k in range(KVH):
            q_k = every_query[:, k * per_head : (k + 1) * per_head, :]
            keys_k = k_cache[:, :, k * HD : (k + 1) * HD]
            vals_k = v_cache[:, :, k * HD : (k + 1) * HD]
            scores = (
                jnp.einsum("nrd,ncd->nrc", q_k, keys_k, preferred_element_type=jnp.float32)
                * scale
            )
            peak = jnp.max(jnp.where(valid, scores, -1e30), axis=-1)
            hi = peak.astype(jnp.bfloat16)
            mid = (peak - hi.astype(jnp.float32)).astype(jnp.bfloat16)
            shard_peak = hi.astype(jnp.float32) + mid.astype(jnp.float32)
            weights = jnp.where(valid, jnp.exp(scores - shard_peak[..., None]), 0.0)
            total_heads.append(jnp.sum(weights, axis=-1))
            mixed_heads.append(
                jnp.einsum(
                    "nrc,ncd->nrd",
                    weights.astype(jnp.bfloat16),
                    vals_k,
                    preferred_element_type=jnp.float32,
                )
            )
            hi_heads.append(hi)
            mid_heads.append(mid)
        stats = jnp.stack(
            [
                jnp.concatenate(total_heads, axis=1),
                jnp.concatenate(hi_heads, axis=1).astype(jnp.float32),
                jnp.concatenate(mid_heads, axis=1).astype(jnp.float32),
            ],
            axis=1,
        )
        stats = jnp.pad(stats, ((0, 0), (0, 8 - 3), (0, HD - rows_q)))
        packed = jnp.concatenate(mixed_heads + [stats], axis=1).astype(jnp.bfloat16)

    with jax.named_scope("partial_exchange"):
        parts = lax.all_to_all(packed, "seq", 0, 0, tiled=True)

    with jax.named_scope("merge_attention"):
        mixed_s = parts[:, :rows_q, :].astype(jnp.float32).reshape(
            seq_count, KVH, STEPS, heads_per, HD
        )
        total_s = parts[:, rows_q, :rows_q].astype(jnp.float32).reshape(
            seq_count, KVH, STEPS, heads_per
        )
        peak_s = (
            parts[:, rows_q + 1, :rows_q].astype(jnp.float32)
            + parts[:, rows_q + 2, :rows_q].astype(jnp.float32)
        ).reshape(seq_count, KVH, STEPS, heads_per)
        tail_scores = (
            jnp.einsum("ktgd,skd->ktgs", q_heads, fresh_key, preferred_element_type=jnp.float32)
            * scale
        )
        tail_valid = (step_ids[None, :] <= step_ids[:, None])[None, :, None, :]
        sink_grid = sink.reshape(KVH, 1, heads_per)
        final = jnp.maximum(
            jnp.maximum(jnp.max(peak_s, axis=0), jnp.max(jnp.where(tail_valid, tail_scores, -1e30), axis=-1)),
            sink_grid,
        )
        shift = jnp.exp(peak_s - final[None])
        tail_w = jnp.where(tail_valid, jnp.exp(tail_scores - final[..., None]), 0.0)
        denom = (
            jnp.sum(total_s * shift, axis=0)
            + jnp.sum(tail_w, axis=-1)
            + jnp.exp(sink_grid - final)
        )
        mixed = jnp.sum(mixed_s * shift[..., None], axis=0) + jnp.einsum(
            "ktgs,skd->ktgd",
            tail_w.astype(jnp.bfloat16),
            fresh_val,
            preferred_element_type=jnp.float32,
        )
        attn = (
            (mixed / denom[..., None]).transpose(1, 0, 2, 3).reshape(STEPS, QH * HD).astype(jnp.bfloat16)
        )

    with jax.named_scope("attention_output"):
        h = (
            x.astype(jnp.float32) + jnp.dot(attn, w_out, preferred_element_type=jnp.float32)
        ).astype(jnp.bfloat16)
        u = normalize(h, moe_gain)

    with jax.named_scope("route"):
        row_ids = jnp.arange(routes.shape[0], dtype=jnp.int32)
        picks = jnp.sum(jnp.where((row_ids == device)[:, None, None], routes, 0), axis=0)
        experts = jnp.arange(E, dtype=jnp.int32)
        onehot = (picks[:, :, None] == experts[None, None, :]).astype(jnp.float32)
        logits = jnp.dot(u, router, preferred_element_type=jnp.float32)
        chosen = jnp.sum(onehot * logits[:, None, :], axis=-1)
        share = jax.nn.softmax(chosen, axis=-1)
        weight_te = jnp.sum(share[:, :, None] * onehot, axis=1)
        named = jnp.any(picks[:, :, None] == experts[None, None, :], axis=1)
        rank = jnp.cumsum(named.astype(jnp.int32), axis=0) - 1
        slots = jnp.arange(MOST, dtype=jnp.int32)
        select = (named[:, :, None] & (rank[:, :, None] == slots[None, None, :])).astype(jnp.float32)
        dispatch = jnp.einsum(
            "tej,tm->ejm", select.astype(jnp.bfloat16), u, preferred_element_type=jnp.float32
        ).astype(jnp.bfloat16)
        per_device = devices // E
        sent_u = jnp.broadcast_to(
            dispatch[:, None], (E, per_device, MOST, D)
        ).reshape(devices, MOST, D)

    with jax.named_scope("token_dispatch"):
        arrived = lax.all_to_all(sent_u, ("req", "seq"), 0, 0, tiled=True)

    with jax.named_scope("expert_quarter"):
        rows_in = arrived.reshape(devices * MOST, D)
        hidden = (
            jax.nn.relu(jnp.dot(rows_in, w_gate, preferred_element_type=jnp.float32))
            * jnp.dot(rows_in, w_up, preferred_element_type=jnp.float32)
        ).astype(jnp.bfloat16)
        produced = (
            jnp.dot(hidden, w_down, preferred_element_type=jnp.float32)
            .astype(jnp.bfloat16)
            .reshape(devices, MOST, D)
        )

    with jax.named_scope("expert_return"):
        returned = lax.all_to_all(produced, ("req", "seq"), 0, 0, tiled=True)

    with jax.named_scope("expert_sum"):
        by_expert = jnp.sum(returned.astype(jnp.float32).reshape(E, per_device, MOST, D), axis=1)
        mix = (weight_te[:, :, None] * select).reshape(STEPS, E * MOST)
        moe = jnp.dot(
            mix, by_expert.reshape(E * MOST, D), precision=lax.Precision.HIGHEST,
            preferred_element_type=jnp.float32,
        )
        out = (h.astype(jnp.float32) + moe).astype(jnp.bfloat16)
    return out[:, None, :]


def solution(mesh):
    in_specs = (
        P(None, ("req", "seq"), None),
        P("req"),
        P("req", "seq", None),
        P("req", "seq", None),
        P(),
        P(),
        P(),
        P(),
        P(),
        P(),
        P(None, ("req", "seq")),
        P(None, ("req", "seq")),
        P(("req", "seq"), None),
        P(),
    )
    out_specs = P(None, ("req", "seq"), None)
    return jax.shard_map(
        on_device, mesh=mesh, in_specs=in_specs, out_specs=out_specs, check_vma=False
    )
```

```python
import jax
import jax.numpy as jnp
from jax import lax
from jax.sharding import PartitionSpec as P

D = 1536
QH = 12
KVH = 2
HD = 128
E = 32
EFF = 768
TOP = 4
STEPS = 4
MOST = 2


def normalize(x, gain):
    xf = x.astype(jnp.float32)
    inv = lax.rsqrt(jnp.mean(xf * xf, axis=-1, keepdims=True) + 1e-05)
    return (xf * inv * gain.astype(jnp.float32)).astype(jnp.bfloat16)


def rotate(x, place):
    half = x.shape[-1] // 2
    index = jnp.arange(half, dtype=jnp.float32)
    inverse = jnp.exp(-jnp.log(1000000.0) * 2.0 * index / x.shape[-1])
    angle = place.astype(jnp.float32)[..., None, None] * inverse
    first = x[..., :half]
    second = x[..., half:]
    cosine = jnp.cos(angle)
    sine = jnp.sin(angle)
    return jnp.concatenate(
        [first * cosine - second * sine, second * cosine + first * sine], axis=-1
    )


def on_device(
    tokens,
    lengths,
    k_cache,
    v_cache,
    attn_gain,
    w_qkv,
    sink,
    w_out,
    moe_gain,
    router,
    w_gate,
    w_up,
    w_down,
    routes,
):
    seq_count = lax.axis_size("seq")
    seq_place = lax.axis_index("seq")
    devices = lax.axis_size(("req", "seq"))
    device = lax.axis_index("req") * seq_count + seq_place
    group_rows = lengths.shape[0]
    local_pos = k_cache.shape[1]
    window = local_pos * seq_count
    heads_per = QH // KVH
    scale = HD ** (-0.5)
    step_ids = jnp.arange(STEPS, dtype=jnp.int32)

    x = tokens[:, 0, :]
    own_len = jnp.sum(jnp.where(jnp.arange(group_rows) == seq_place, lengths, 0))
    with jax.named_scope("qkv_projection"):
        a = normalize(x, attn_gain)
        proj = jnp.dot(a, w_qkv, preferred_element_type=jnp.float32)
        place = own_len + step_ids
        query = rotate(proj[:, : QH * HD].reshape(STEPS, QH, HD), place).astype(jnp.bfloat16)
    with jax.named_scope("fresh_key_value"):
        fresh_key = rotate(
            proj[:, QH * HD : (QH + KVH) * HD].reshape(STEPS, KVH, HD), place
        ).astype(jnp.bfloat16)
        fresh_val = proj[:, (QH + KVH) * HD :].reshape(STEPS, KVH, HD).astype(jnp.bfloat16)

    per_head = STEPS * heads_per
    rows_q = KVH * per_head
    q_heads = query.reshape(STEPS, KVH, heads_per, HD).transpose(1, 0, 2, 3)
    with jax.named_scope("query_exchange"):
        sent_q = jnp.broadcast_to(q_heads.reshape(1, rows_q, HD), (seq_count, rows_q, HD))
        every_query = lax.all_to_all(sent_q, "seq", 0, 0, tiled=True)

    with jax.named_scope("slot_attention"):
        key_slot = seq_place * local_pos + jnp.arange(local_pos, dtype=jnp.int32)
        back = jnp.mod(lengths[:, None] - 1 - key_slot[None, :], window)
        row_step = jnp.arange(per_head, dtype=jnp.int32) // heads_per
        reach = jnp.minimum(lengths[:, None], window - 1 - row_step[None, :])
        valid = back[:, None, :] < reach[:, :, None]
        mixed_heads, total_heads, hi_heads, mid_heads = [], [], [], []
        halves = lax.optimization_barrier(
            tuple(c[:, :, k * HD : (k + 1) * HD] for c in (k_cache, v_cache) for k in range(KVH))
        )
        for k in range(KVH):
            q_k = every_query[:, k * per_head : (k + 1) * per_head, :]
            keys_k = halves[k]
            vals_k = halves[KVH + k]
            scores = (
                jnp.einsum("nrd,ncd->nrc", q_k, keys_k, preferred_element_type=jnp.float32)
                * scale
            )
            peak = jnp.max(jnp.where(valid, scores, -1e30), axis=-1)
            hi = peak.astype(jnp.bfloat16)
            mid = (peak - hi.astype(jnp.float32)).astype(jnp.bfloat16)
            shard_peak = hi.astype(jnp.float32) + mid.astype(jnp.float32)
            weights = jnp.where(valid, jnp.exp(scores - shard_peak[..., None]), 0.0)
            total_heads.append(jnp.sum(weights, axis=-1))
            mixed_heads.append(
                jnp.einsum(
                    "nrc,ncd->nrd",
                    weights.astype(jnp.bfloat16),
                    vals_k,
                    preferred_element_type=jnp.float32,
                )
            )
            hi_heads.append(hi)
            mid_heads.append(mid)
        stats = jnp.stack(
            [
                jnp.concatenate(total_heads, axis=1),
                jnp.concatenate(hi_heads, axis=1).astype(jnp.float32),
                jnp.concatenate(mid_heads, axis=1).astype(jnp.float32),
            ],
            axis=1,
        )
        stats = jnp.pad(stats, ((0, 0), (0, 8 - 3), (0, HD - rows_q)))
        packed = jnp.concatenate(mixed_heads + [stats], axis=1).astype(jnp.bfloat16)

    with jax.named_scope("partial_exchange"):
        parts = lax.all_to_all(packed, "seq", 0, 0, tiled=True)

    with jax.named_scope("merge_attention"):
        mixed_s = parts[:, :rows_q, :].astype(jnp.float32).reshape(
            seq_count, KVH, STEPS, heads_per, HD
        )
        total_s = parts[:, rows_q, :rows_q].astype(jnp.float32).reshape(
            seq_count, KVH, STEPS, heads_per
        )
        peak_s = (
            parts[:, rows_q + 1, :rows_q].astype(jnp.float32)
            + parts[:, rows_q + 2, :rows_q].astype(jnp.float32)
        ).reshape(seq_count, KVH, STEPS, heads_per)
        tail_scores = (
            jnp.einsum("ktgd,skd->ktgs", q_heads, fresh_key, preferred_element_type=jnp.float32)
            * scale
        )
        tail_valid = (step_ids[None, :] <= step_ids[:, None])[None, :, None, :]
        sink_grid = sink.reshape(KVH, 1, heads_per)
        final = jnp.maximum(
            jnp.maximum(jnp.max(peak_s, axis=0), jnp.max(jnp.where(tail_valid, tail_scores, -1e30), axis=-1)),
            sink_grid,
        )
        shift = jnp.exp(peak_s - final[None])
        tail_w = jnp.where(tail_valid, jnp.exp(tail_scores - final[..., None]), 0.0)
        denom = (
            jnp.sum(total_s * shift, axis=0)
            + jnp.sum(tail_w, axis=-1)
            + jnp.exp(sink_grid - final)
        )
        mixed = jnp.sum(mixed_s * shift[..., None], axis=0) + jnp.einsum(
            "ktgs,skd->ktgd",
            tail_w.astype(jnp.bfloat16),
            fresh_val,
            preferred_element_type=jnp.float32,
        )
        attn = (
            (mixed / denom[..., None]).transpose(1, 0, 2, 3).reshape(STEPS, QH * HD).astype(jnp.bfloat16)
        )

    with jax.named_scope("attention_output"):
        h = (
            x.astype(jnp.float32) + jnp.dot(attn, w_out, preferred_element_type=jnp.float32)
        ).astype(jnp.bfloat16)
        u = normalize(h, moe_gain)

    with jax.named_scope("route"):
        row_ids = jnp.arange(routes.shape[0], dtype=jnp.int32)
        picks = jnp.sum(jnp.where((row_ids == device)[:, None, None], routes, 0), axis=0)
        experts = jnp.arange(E, dtype=jnp.int32)
        onehot = (picks[:, :, None] == experts[None, None, :]).astype(jnp.float32)
        logits = jnp.dot(u, router, preferred_element_type=jnp.float32)
        chosen = jnp.sum(onehot * logits[:, None, :], axis=-1)
        share = jax.nn.softmax(chosen, axis=-1)
        weight_te = jnp.sum(share[:, :, None] * onehot, axis=1)
        named = jnp.any(picks[:, :, None] == experts[None, None, :], axis=1)
        rank = jnp.cumsum(named.astype(jnp.int32), axis=0) - 1
        slots = jnp.arange(MOST, dtype=jnp.int32)
        select = (named[:, :, None] & (rank[:, :, None] == slots[None, None, :])).astype(jnp.float32)
        dispatch = jnp.einsum(
            "tej,tm->ejm", select.astype(jnp.bfloat16), u, preferred_element_type=jnp.float32
        ).astype(jnp.bfloat16)
        per_device = devices // E
        sent_u = jnp.broadcast_to(
            dispatch[:, None], (E, per_device, MOST, D)
        ).reshape(devices, MOST, D)

    with jax.named_scope("token_dispatch"):
        arrived = lax.all_to_all(sent_u, ("req", "seq"), 0, 0, tiled=True)

    with jax.named_scope("expert_quarter"):
        hidden = (
            jax.nn.relu(jnp.einsum("sjm,mf->sjf", arrived, w_gate, preferred_element_type=jnp.float32))
            * jnp.einsum("sjm,mf->sjf", arrived, w_up, preferred_element_type=jnp.float32)
        ).astype(jnp.bfloat16)
        produced = jnp.einsum(
            "sjf,fm->sjm", hidden, w_down, preferred_element_type=jnp.float32
        ).astype(jnp.bfloat16)

    with jax.named_scope("expert_return"):
        returned = lax.all_to_all(produced, ("req", "seq"), 0, 0, tiled=True)

    with jax.named_scope("expert_sum"):
        by_expert = jnp.sum(returned.astype(jnp.float32).reshape(E, per_device, MOST, D), axis=1)
        mix = (weight_te[:, :, None] * select).reshape(STEPS, E * MOST)
        moe = jnp.dot(
            mix, by_expert.reshape(E * MOST, D), precision=lax.Precision.HIGHEST,
            preferred_element_type=jnp.float32,
        )
        out = (h.astype(jnp.float32) + moe).astype(jnp.bfloat16)
    return out[:, None, :]


def solution(mesh):
    in_specs = (
        P(None, ("req", "seq"), None),
        P("req"),
        P("req", "seq", None),
        P("req", "seq", None),
        P(),
        P(),
        P(),
        P(),
        P(),
        P(),
        P(None, ("req", "seq")),
        P(None, ("req", "seq")),
        P(("req", "seq"), None),
        P(),
    )
    out_specs = P(None, ("req", "seq"), None)
    return jax.shard_map(
        on_device, mesh=mesh, in_specs=in_specs, out_specs=out_specs, check_vma=False
    )
```

```python
import jax
import jax.numpy as jnp
from jax import lax
from jax.sharding import PartitionSpec as P

D = 1536
QH = 12
KVH = 2
HD = 128
E = 32
EFF = 768
TOP = 4
STEPS = 4
MOST = 2


def normalize(x, gain):
    xf = x.astype(jnp.float32)
    inv = lax.rsqrt(jnp.mean(xf * xf, axis=-1, keepdims=True) + 1e-05)
    return (xf * inv * gain.astype(jnp.float32)).astype(jnp.bfloat16)


def rotate(x, place):
    half = x.shape[-1] // 2
    index = jnp.arange(half, dtype=jnp.float32)
    inverse = jnp.exp(-jnp.log(1000000.0) * 2.0 * index / x.shape[-1])
    angle = place.astype(jnp.float32)[..., None, None] * inverse
    first = x[..., :half]
    second = x[..., half:]
    cosine = jnp.cos(angle)
    sine = jnp.sin(angle)
    return jnp.concatenate(
        [first * cosine - second * sine, second * cosine + first * sine], axis=-1
    )


def on_device(
    tokens,
    lengths,
    k_cache,
    v_cache,
    attn_gain,
    w_qkv,
    sink,
    w_out,
    moe_gain,
    router,
    w_gate,
    w_up,
    w_down,
    routes,
):
    seq_count = lax.axis_size("seq")
    seq_place = lax.axis_index("seq")
    devices = lax.axis_size(("req", "seq"))
    device = lax.axis_index("req") * seq_count + seq_place
    group_rows = lengths.shape[0]
    local_pos = k_cache.shape[1]
    window = local_pos * seq_count
    heads_per = QH // KVH
    scale = HD ** (-0.5)
    step_ids = jnp.arange(STEPS, dtype=jnp.int32)

    x = tokens[:, 0, :]
    own_len = jnp.sum(jnp.where(jnp.arange(group_rows) == seq_place, lengths, 0))
    with jax.named_scope("qkv_projection"):
        a = normalize(x, attn_gain)
        proj = jnp.dot(a, w_qkv, preferred_element_type=jnp.float32)
        place = own_len + step_ids
        query = rotate(proj[:, : QH * HD].reshape(STEPS, QH, HD), place).astype(jnp.bfloat16)
    with jax.named_scope("fresh_key_value"):
        fresh_key = rotate(
            proj[:, QH * HD : (QH + KVH) * HD].reshape(STEPS, KVH, HD), place
        ).astype(jnp.bfloat16)
        fresh_val = proj[:, (QH + KVH) * HD :].reshape(STEPS, KVH, HD).astype(jnp.bfloat16)

    per_head = STEPS * heads_per
    rows_q = KVH * per_head
    q_heads = query.reshape(STEPS, KVH, heads_per, HD).transpose(1, 0, 2, 3)
    with jax.named_scope("query_exchange"):
        sent_q = jnp.broadcast_to(q_heads.reshape(1, rows_q, HD), (seq_count, rows_q, HD))
        every_query = lax.all_to_all(sent_q, "seq", 0, 0, tiled=True)

    with jax.named_scope("slot_attention"):
        key_slot = seq_place * local_pos + jnp.arange(local_pos, dtype=jnp.int32)
        back = jnp.mod(lengths[:, None] - 1 - key_slot[None, :], window)
        row_ids = jnp.arange(rows_q, dtype=jnp.int32)
        row_head = row_ids // per_head
        row_step = (row_ids % per_head) // heads_per
        reach = jnp.minimum(lengths[:, None], window - 1 - row_step[None, :])
        valid = back[:, None, :] < reach[:, :, None]
        lane_head = jnp.arange(KVH * HD, dtype=jnp.int32) // HD
        own_half = row_head[None, :, None] == lane_head[None, None, :]
        q_spread = jnp.where(
            own_half, jnp.concatenate([every_query] * KVH, axis=-1), jnp.zeros((), jnp.bfloat16)
        )
        scores = (
            jnp.einsum("nre,nce->nrc", q_spread, k_cache, preferred_element_type=jnp.float32)
            * scale
        )
        peak = jnp.max(jnp.where(valid, scores, -1e30), axis=-1)
        hi = peak.astype(jnp.bfloat16)
        mid = (peak - hi.astype(jnp.float32)).astype(jnp.bfloat16)
        shard_peak = hi.astype(jnp.float32) + mid.astype(jnp.float32)
        weights = jnp.where(valid, jnp.exp(scores - shard_peak[..., None]), 0.0)
        total_heads = [jnp.sum(weights, axis=-1)]
        hi_heads, mid_heads = [hi], [mid]
        mixed_heads = []
        for k in range(KVH):
            vals_k = v_cache[:, :, k * HD : (k + 1) * HD]
            mixed_heads.append(
                jnp.einsum(
                    "nrc,ncd->nrd",
                    weights[:, k * per_head : (k + 1) * per_head].astype(jnp.bfloat16),
                    vals_k,
                    preferred_element_type=jnp.float32,
                )
            )
        stats = jnp.stack(
            [
                jnp.concatenate(total_heads, axis=1),
                jnp.concatenate(hi_heads, axis=1).astype(jnp.float32),
                jnp.concatenate(mid_heads, axis=1).astype(jnp.float32),
            ],
            axis=1,
        )
        stats = jnp.pad(stats, ((0, 0), (0, 8 - 3), (0, HD - rows_q)))
        packed = jnp.concatenate(mixed_heads + [stats], axis=1).astype(jnp.bfloat16)

    with jax.named_scope("partial_exchange"):
        parts = lax.all_to_all(packed, "seq", 0, 0, tiled=True)

    with jax.named_scope("merge_attention"):
        mixed_s = parts[:, :rows_q, :].astype(jnp.float32).reshape(
            seq_count, KVH, STEPS, heads_per, HD
        )
        total_s = parts[:, rows_q, :rows_q].astype(jnp.float32).reshape(
            seq_count, KVH, STEPS, heads_per
        )
        peak_s = (
            parts[:, rows_q + 1, :rows_q].astype(jnp.float32)
            + parts[:, rows_q + 2, :rows_q].astype(jnp.float32)
        ).reshape(seq_count, KVH, STEPS, heads_per)
        tail_scores = (
            jnp.einsum("ktgd,skd->ktgs", q_heads, fresh_key, preferred_element_type=jnp.float32)
            * scale
        )
        tail_valid = (step_ids[None, :] <= step_ids[:, None])[None, :, None, :]
        sink_grid = sink.reshape(KVH, 1, heads_per)
        final = jnp.maximum(
            jnp.maximum(jnp.max(peak_s, axis=0), jnp.max(jnp.where(tail_valid, tail_scores, -1e30), axis=-1)),
            sink_grid,
        )
        shift = jnp.exp(peak_s - final[None])
        tail_w = jnp.where(tail_valid, jnp.exp(tail_scores - final[..., None]), 0.0)
        denom = (
            jnp.sum(total_s * shift, axis=0)
            + jnp.sum(tail_w, axis=-1)
            + jnp.exp(sink_grid - final)
        )
        mixed = jnp.sum(mixed_s * shift[..., None], axis=0) + jnp.einsum(
            "ktgs,skd->ktgd",
            tail_w.astype(jnp.bfloat16),
            fresh_val,
            preferred_element_type=jnp.float32,
        )
        attn = (
            (mixed / denom[..., None]).transpose(1, 0, 2, 3).reshape(STEPS, QH * HD).astype(jnp.bfloat16)
        )

    with jax.named_scope("attention_output"):
        h = (
            x.astype(jnp.float32) + jnp.dot(attn, w_out, preferred_element_type=jnp.float32)
        ).astype(jnp.bfloat16)
        u = normalize(h, moe_gain)

    with jax.named_scope("route"):
        row_ids = jnp.arange(routes.shape[0], dtype=jnp.int32)
        picks = jnp.sum(jnp.where((row_ids == device)[:, None, None], routes, 0), axis=0)
        experts = jnp.arange(E, dtype=jnp.int32)
        onehot = (picks[:, :, None] == experts[None, None, :]).astype(jnp.float32)
        logits = jnp.dot(u, router, preferred_element_type=jnp.float32)
        chosen = jnp.sum(onehot * logits[:, None, :], axis=-1)
        share = jax.nn.softmax(chosen, axis=-1)
        weight_te = jnp.sum(share[:, :, None] * onehot, axis=1)
        named = jnp.any(picks[:, :, None] == experts[None, None, :], axis=1)
        rank = jnp.cumsum(named.astype(jnp.int32), axis=0) - 1
        slots = jnp.arange(MOST, dtype=jnp.int32)
        select = (named[:, :, None] & (rank[:, :, None] == slots[None, None, :])).astype(jnp.float32)
        dispatch = jnp.einsum(
            "tej,tm->ejm", select.astype(jnp.bfloat16), u, preferred_element_type=jnp.float32
        ).astype(jnp.bfloat16)
        per_device = devices // E
        sent_u = jnp.broadcast_to(
            dispatch[:, None], (E, per_device, MOST, D)
        ).reshape(devices, MOST, D)

    with jax.named_scope("token_dispatch"):
        arrived = lax.all_to_all(sent_u, ("req", "seq"), 0, 0, tiled=True)

    with jax.named_scope("expert_quarter"):
        rows_in = arrived.reshape(devices * MOST, D)
        hidden = (
            jax.nn.relu(jnp.dot(rows_in, w_gate, preferred_element_type=jnp.float32))
            * jnp.dot(rows_in, w_up, preferred_element_type=jnp.float32)
        ).astype(jnp.bfloat16)
        produced = (
            jnp.dot(hidden, w_down, preferred_element_type=jnp.float32)
            .astype(jnp.bfloat16)
            .reshape(devices, MOST, D)
        )

    with jax.named_scope("expert_return"):
        returned = lax.all_to_all(produced, ("req", "seq"), 0, 0, tiled=True)

    with jax.named_scope("expert_sum"):
        by_expert = jnp.sum(returned.astype(jnp.float32).reshape(E, per_device, MOST, D), axis=1)
        mix = (weight_te[:, :, None] * select).reshape(STEPS, E * MOST)
        moe = jnp.dot(
            mix, by_expert.reshape(E * MOST, D), precision=lax.Precision.HIGHEST,
            preferred_element_type=jnp.float32,
        )
        out = (h.astype(jnp.float32) + moe).astype(jnp.bfloat16)
    return out[:, None, :]


def solution(mesh):
    in_specs = (
        P(None, ("req", "seq"), None),
        P("req"),
        P("req", "seq", None),
        P("req", "seq", None),
        P(),
        P(),
        P(),
        P(),
        P(),
        P(),
        P(None, ("req", "seq")),
        P(None, ("req", "seq")),
        P(("req", "seq"), None),
        P(),
    )
    out_specs = P(None, ("req", "seq"), None)
    return jax.shard_map(
        on_device, mesh=mesh, in_specs=in_specs, out_specs=out_specs, check_vma=False
    )
```

```python
import jax
import jax.numpy as jnp
from jax import lax
from jax.experimental import pallas as pl
from jax.experimental.pallas import tpu as pltpu
from jax.sharding import PartitionSpec as P

D = 1536
QH = 12
KVH = 2
HD = 128
E = 32
EFF = 768
TOP = 4
STEPS = 4
MOST = 2


def normalize(x, gain):
    xf = x.astype(jnp.float32)
    inv = lax.rsqrt(jnp.mean(xf * xf, axis=-1, keepdims=True) + 1e-05)
    return (xf * inv * gain.astype(jnp.float32)).astype(jnp.bfloat16)


def rotate(x, place):
    half = x.shape[-1] // 2
    index = jnp.arange(half, dtype=jnp.float32)
    inverse = jnp.exp(-jnp.log(1000000.0) * 2.0 * index / x.shape[-1])
    angle = place.astype(jnp.float32)[..., None, None] * inverse
    first = x[..., :half]
    second = x[..., half:]
    cosine = jnp.cos(angle)
    sine = jnp.sin(angle)
    return jnp.concatenate(
        [first * cosine - second * sine, second * cosine + first * sine], axis=-1
    )


def expert_kernel(rows_ref, gate_ref, up_ref, down_ref, out_ref):
    rows = rows_ref[...]
    gate = jnp.dot(rows, gate_ref[...], preferred_element_type=jnp.float32)
    up = jnp.dot(rows, up_ref[...], preferred_element_type=jnp.float32)
    hidden = (jnp.maximum(gate, 0.0) * up).astype(jnp.bfloat16)
    out_ref[...] = jnp.dot(hidden, down_ref[...], preferred_element_type=jnp.float32).astype(
        out_ref.dtype
    )


def expert_quarter(rows, w_gate, w_up, w_down):
    count, width = rows.shape
    units = w_gate.shape[1]
    return pl.pallas_call(
        expert_kernel,
        out_shape=jax.ShapeDtypeStruct((count, width), jnp.bfloat16),
        in_specs=[pl.BlockSpec(memory_space=pltpu.VMEM)] * 4,
        out_specs=pl.BlockSpec(memory_space=pltpu.VMEM),
        cost_estimate=pl.CostEstimate(
            flops=6 * count * width * units,
            transcendentals=0,
            bytes_accessed=2 * (3 * width * units + 2 * count * width),
        ),
    )(rows, w_gate, w_up, w_down)


def on_device(
    tokens,
    lengths,
    k_cache,
    v_cache,
    attn_gain,
    w_qkv,
    sink,
    w_out,
    moe_gain,
    router,
    w_gate,
    w_up,
    w_down,
    routes,
):
    seq_count = lax.axis_size("seq")
    seq_place = lax.axis_index("seq")
    devices = lax.axis_size(("req", "seq"))
    device = lax.axis_index("req") * seq_count + seq_place
    group_rows = lengths.shape[0]
    local_pos = k_cache.shape[1]
    window = local_pos * seq_count
    heads_per = QH // KVH
    scale = HD ** (-0.5)
    step_ids = jnp.arange(STEPS, dtype=jnp.int32)

    x = tokens[:, 0, :]
    own_len = jnp.sum(jnp.where(jnp.arange(group_rows) == seq_place, lengths, 0))
    with jax.named_scope("qkv_projection"):
        a = normalize(x, attn_gain)
        proj = jnp.dot(a, w_qkv, preferred_element_type=jnp.float32)
        place = own_len + step_ids
        query = rotate(proj[:, : QH * HD].reshape(STEPS, QH, HD), place).astype(jnp.bfloat16)
    with jax.named_scope("fresh_key_value"):
        fresh_key = rotate(
            proj[:, QH * HD : (QH + KVH) * HD].reshape(STEPS, KVH, HD), place
        ).astype(jnp.bfloat16)
        fresh_val = proj[:, (QH + KVH) * HD :].reshape(STEPS, KVH, HD).astype(jnp.bfloat16)

    per_head = STEPS * heads_per
    rows_q = KVH * per_head
    q_heads = query.reshape(STEPS, KVH, heads_per, HD).transpose(1, 0, 2, 3)
    with jax.named_scope("query_exchange"):
        sent_q = jnp.broadcast_to(q_heads.reshape(1, rows_q, HD), (seq_count, rows_q, HD))
        every_query = lax.all_to_all(sent_q, "seq", 0, 0, tiled=True)

    with jax.named_scope("slot_attention"):
        key_slot = seq_place * local_pos + jnp.arange(local_pos, dtype=jnp.int32)
        back = jnp.mod(lengths[:, None] - 1 - key_slot[None, :], window)
        row_ids = jnp.arange(rows_q, dtype=jnp.int32)
        row_head = row_ids // per_head
        row_step = (row_ids % per_head) // heads_per
        reach = jnp.minimum(lengths[:, None], window - 1 - row_step[None, :])
        valid = back[:, None, :] < reach[:, :, None]
        lane_head = jnp.arange(KVH * HD, dtype=jnp.int32) // HD
        own_half = row_head[None, :, None] == lane_head[None, None, :]
        q_spread = jnp.where(
            own_half, jnp.concatenate([every_query] * KVH, axis=-1), jnp.zeros((), jnp.bfloat16)
        )
        scores = (
            jnp.einsum("nre,nce->nrc", q_spread, k_cache, preferred_element_type=jnp.float32)
            * scale
        )
        peak = jnp.max(jnp.where(valid, scores, -1e30), axis=-1)
        hi = peak.astype(jnp.bfloat16)
        mid = (peak - hi.astype(jnp.float32)).astype(jnp.bfloat16)
        shard_peak = hi.astype(jnp.float32) + mid.astype(jnp.float32)
        weights = jnp.where(valid, jnp.exp(scores - shard_peak[..., None]), 0.0)
        total_heads = [jnp.sum(weights, axis=-1)]
        hi_heads, mid_heads = [hi], [mid]
        mixed_heads = []
        for k in range(KVH):
            vals_k = v_cache[:, :, k * HD : (k + 1) * HD]
            mixed_heads.append(
                jnp.einsum(
                    "nrc,ncd->nrd",
                    weights[:, k * per_head : (k + 1) * per_head].astype(jnp.bfloat16),
                    vals_k,
                    preferred_element_type=jnp.float32,
                )
            )
        stats = jnp.stack(
            [
                jnp.concatenate(total_heads, axis=1),
                jnp.concatenate(hi_heads, axis=1).astype(jnp.float32),
                jnp.concatenate(mid_heads, axis=1).astype(jnp.float32),
            ],
            axis=1,
        )
        stats = jnp.pad(stats, ((0, 0), (0, 8 - 3), (0, HD - rows_q)))
        packed = jnp.concatenate(mixed_heads + [stats], axis=1).astype(jnp.bfloat16)

    with jax.named_scope("partial_exchange"):
        parts = lax.all_to_all(packed, "seq", 0, 0, tiled=True)

    with jax.named_scope("merge_attention"):
        mixed_s = parts[:, :rows_q, :].astype(jnp.float32).reshape(
            seq_count, KVH, STEPS, heads_per, HD
        )
        total_s = parts[:, rows_q, :rows_q].astype(jnp.float32).reshape(
            seq_count, KVH, STEPS, heads_per
        )
        peak_s = (
            parts[:, rows_q + 1, :rows_q].astype(jnp.float32)
            + parts[:, rows_q + 2, :rows_q].astype(jnp.float32)
        ).reshape(seq_count, KVH, STEPS, heads_per)
        tail_scores = (
            jnp.einsum("ktgd,skd->ktgs", q_heads, fresh_key, preferred_element_type=jnp.float32)
            * scale
        )
        tail_valid = (step_ids[None, :] <= step_ids[:, None])[None, :, None, :]
        sink_grid = sink.reshape(KVH, 1, heads_per)
        final = jnp.maximum(
            jnp.maximum(jnp.max(peak_s, axis=0), jnp.max(jnp.where(tail_valid, tail_scores, -1e30), axis=-1)),
            sink_grid,
        )
        shift = jnp.exp(peak_s - final[None])
        tail_w = jnp.where(tail_valid, jnp.exp(tail_scores - final[..., None]), 0.0)
        denom = (
            jnp.sum(total_s * shift, axis=0)
            + jnp.sum(tail_w, axis=-1)
            + jnp.exp(sink_grid - final)
        )
        mixed = jnp.sum(mixed_s * shift[..., None], axis=0) + jnp.einsum(
            "ktgs,skd->ktgd",
            tail_w.astype(jnp.bfloat16),
            fresh_val,
            preferred_element_type=jnp.float32,
        )
        attn = (
            (mixed / denom[..., None]).transpose(1, 0, 2, 3).reshape(STEPS, QH * HD).astype(jnp.bfloat16)
        )

    with jax.named_scope("attention_output"):
        h = (
            x.astype(jnp.float32) + jnp.dot(attn, w_out, preferred_element_type=jnp.float32)
        ).astype(jnp.bfloat16)
        u = normalize(h, moe_gain)

    with jax.named_scope("route"):
        row_ids = jnp.arange(routes.shape[0], dtype=jnp.int32)
        picks = jnp.sum(jnp.where((row_ids == device)[:, None, None], routes, 0), axis=0)
        experts = jnp.arange(E, dtype=jnp.int32)
        onehot = (picks[:, :, None] == experts[None, None, :]).astype(jnp.float32)
        logits = jnp.dot(u, router, preferred_element_type=jnp.float32)
        chosen = jnp.sum(onehot * logits[:, None, :], axis=-1)
        share = jax.nn.softmax(chosen, axis=-1)
        weight_te = jnp.sum(share[:, :, None] * onehot, axis=1)
        named = jnp.any(picks[:, :, None] == experts[None, None, :], axis=1)
        rank = jnp.cumsum(named.astype(jnp.int32), axis=0) - 1
        slots = jnp.arange(MOST, dtype=jnp.int32)
        select = (named[:, :, None] & (rank[:, :, None] == slots[None, None, :])).astype(jnp.float32)
        dispatch = jnp.einsum(
            "tej,tm->ejm", select.astype(jnp.bfloat16), u, preferred_element_type=jnp.float32
        ).astype(jnp.bfloat16)
        per_device = devices // E
        sent_u = jnp.broadcast_to(
            dispatch[:, None], (E, per_device, MOST, D)
        ).reshape(devices, MOST, D)

    with jax.named_scope("token_dispatch"):
        arrived = lax.all_to_all(sent_u, ("req", "seq"), 0, 0, tiled=True)

    with jax.named_scope("expert_quarter"):
        rows_in = arrived.reshape(devices * MOST, D)
        produced = expert_quarter(rows_in, w_gate, w_up, w_down).reshape(devices, MOST, D)

    with jax.named_scope("expert_return"):
        returned = lax.all_to_all(produced, ("req", "seq"), 0, 0, tiled=True)

    with jax.named_scope("expert_sum"):
        by_expert = jnp.sum(returned.astype(jnp.float32).reshape(E, per_device, MOST, D), axis=1)
        mix = (weight_te[:, :, None] * select).reshape(STEPS, E * MOST)
        moe = jnp.dot(
            mix, by_expert.reshape(E * MOST, D), precision=lax.Precision.HIGHEST,
            preferred_element_type=jnp.float32,
        )
        out = (h.astype(jnp.float32) + moe).astype(jnp.bfloat16)
    return out[:, None, :]


def solution(mesh):
    in_specs = (
        P(None, ("req", "seq"), None),
        P("req"),
        P("req", "seq", None),
        P("req", "seq", None),
        P(),
        P(),
        P(),
        P(),
        P(),
        P(),
        P(None, ("req", "seq")),
        P(None, ("req", "seq")),
        P(("req", "seq"), None),
        P(),
    )
    out_specs = P(None, ("req", "seq"), None)
    return jax.shard_map(
        on_device, mesh=mesh, in_specs=in_specs, out_specs=out_specs, check_vma=False
    )
```

```python
import jax
import jax.numpy as jnp
from jax import lax
from jax.sharding import PartitionSpec as P

D = 1536
QH = 12
KVH = 2
HD = 128
E = 32
EFF = 768
TOP = 4
STEPS = 4
MOST = 2


def normalize(x, gain):
    xf = x.astype(jnp.float32)
    inv = lax.rsqrt(jnp.mean(xf * xf, axis=-1, keepdims=True) + 1e-05)
    return (xf * inv * gain.astype(jnp.float32)).astype(jnp.bfloat16)


def rotate(x, place):
    half = x.shape[-1] // 2
    index = jnp.arange(half, dtype=jnp.float32)
    inverse = jnp.exp(-jnp.log(1000000.0) * 2.0 * index / x.shape[-1])
    angle = place.astype(jnp.float32)[..., None, None] * inverse
    first = x[..., :half]
    second = x[..., half:]
    cosine = jnp.cos(angle)
    sine = jnp.sin(angle)
    return jnp.concatenate(
        [first * cosine - second * sine, second * cosine + first * sine], axis=-1
    )


def on_device(
    tokens,
    lengths,
    k_cache,
    v_cache,
    attn_gain,
    w_qkv,
    sink,
    w_out,
    moe_gain,
    router,
    w_gate,
    w_up,
    w_down,
    routes,
):
    seq_count = lax.axis_size("seq")
    seq_place = lax.axis_index("seq")
    devices = lax.axis_size(("req", "seq"))
    device = lax.axis_index("req") * seq_count + seq_place
    group_rows = lengths.shape[0]
    local_pos = k_cache.shape[1]
    window = local_pos * seq_count
    heads_per = QH // KVH
    scale = HD ** (-0.5)
    step_ids = jnp.arange(STEPS, dtype=jnp.int32)

    x = tokens[:, 0, :]
    own_len = jnp.sum(jnp.where(jnp.arange(group_rows) == seq_place, lengths, 0))
    with jax.named_scope("qkv_projection"):
        a = normalize(x, attn_gain)
        proj = jnp.dot(a, w_qkv, preferred_element_type=jnp.float32)
        place = own_len + step_ids
        query = rotate(proj[:, : QH * HD].reshape(STEPS, QH, HD), place).astype(jnp.bfloat16)
    with jax.named_scope("fresh_key_value"):
        fresh_key = rotate(
            proj[:, QH * HD : (QH + KVH) * HD].reshape(STEPS, KVH, HD), place
        ).astype(jnp.bfloat16)
        fresh_val = proj[:, (QH + KVH) * HD :].reshape(STEPS, KVH, HD).astype(jnp.bfloat16)

    per_head = STEPS * heads_per
    rows_q = KVH * per_head
    q_heads = query.reshape(STEPS, KVH, heads_per, HD).transpose(1, 0, 2, 3)
    with jax.named_scope("query_exchange"):
        sent_q = jnp.broadcast_to(q_heads.reshape(1, rows_q, HD), (seq_count, rows_q, HD))
        every_query = lax.all_to_all(sent_q, "seq", 0, 0, tiled=True)

    with jax.named_scope("slot_attention"):
        key_slot = seq_place * local_pos + jnp.arange(local_pos, dtype=jnp.int32)
        back = jnp.mod(lengths[:, None] - 1 - key_slot[None, :], window)
        row_ids = jnp.arange(rows_q, dtype=jnp.int32)
        row_head = row_ids // per_head
        row_step = (row_ids % per_head) // heads_per
        reach = jnp.minimum(lengths[:, None], window - 1 - row_step[None, :])
        valid = back[:, None, :] < reach[:, :, None]
        lane_head = jnp.arange(KVH * HD, dtype=jnp.int32) // HD
        own_half = row_head[None, :, None] == lane_head[None, None, :]
        q_spread = jnp.where(
            own_half, jnp.concatenate([every_query] * KVH, axis=-1), jnp.zeros((), jnp.bfloat16)
        )
        scores = (
            jnp.einsum("nre,nce->nrc", q_spread, k_cache, preferred_element_type=jnp.float32)
            * scale
        )
        peak = jnp.max(jnp.where(valid, scores, -1e30), axis=-1)
        hi = peak.astype(jnp.bfloat16)
        mid = (peak - hi.astype(jnp.float32)).astype(jnp.bfloat16)
        shard_peak = hi.astype(jnp.float32) + mid.astype(jnp.float32)
        weights = jnp.where(valid, jnp.exp(scores - shard_peak[..., None]), 0.0)
        total_heads = [jnp.sum(weights, axis=-1)]
        hi_heads, mid_heads = [hi], [mid]
        mixed_heads = []
        for k in range(KVH):
            vals_k = v_cache[:, :, k * HD : (k + 1) * HD]
            mixed_heads.append(
                jnp.einsum(
                    "nrc,ncd->nrd",
                    weights[:, k * per_head : (k + 1) * per_head].astype(jnp.bfloat16),
                    vals_k,
                    preferred_element_type=jnp.float32,
                )
            )
        stats = jnp.stack(
            [
                jnp.concatenate(total_heads, axis=1),
                jnp.concatenate(hi_heads, axis=1).astype(jnp.float32),
                jnp.concatenate(mid_heads, axis=1).astype(jnp.float32),
            ],
            axis=1,
        )
        stats = jnp.pad(stats, ((0, 0), (0, 8 - 3), (0, HD - rows_q)))
        packed = jnp.concatenate(mixed_heads + [stats], axis=1).astype(jnp.bfloat16)

    with jax.named_scope("partial_exchange"):
        parts = lax.all_to_all(packed, "seq", 0, 0, tiled=True)

    with jax.named_scope("merge_attention"):
        mixed_s = parts[:, :rows_q, :].astype(jnp.float32).reshape(
            seq_count, KVH, STEPS, heads_per, HD
        )
        total_s = parts[:, rows_q, :rows_q].astype(jnp.float32).reshape(
            seq_count, KVH, STEPS, heads_per
        )
        peak_s = (
            parts[:, rows_q + 1, :rows_q].astype(jnp.float32)
            + parts[:, rows_q + 2, :rows_q].astype(jnp.float32)
        ).reshape(seq_count, KVH, STEPS, heads_per)
        tail_scores = (
            jnp.einsum("ktgd,skd->ktgs", q_heads, fresh_key, preferred_element_type=jnp.float32)
            * scale
        )
        tail_valid = (step_ids[None, :] <= step_ids[:, None])[None, :, None, :]
        sink_grid = sink.reshape(KVH, 1, heads_per)
        final = jnp.maximum(
            jnp.maximum(jnp.max(peak_s, axis=0), jnp.max(jnp.where(tail_valid, tail_scores, -1e30), axis=-1)),
            sink_grid,
        )
        shift = jnp.exp(peak_s - final[None])
        tail_w = jnp.where(tail_valid, jnp.exp(tail_scores - final[..., None]), 0.0)
        denom = (
            jnp.sum(total_s * shift, axis=0)
            + jnp.sum(tail_w, axis=-1)
            + jnp.exp(sink_grid - final)
        )
        mixed = jnp.sum(mixed_s * shift[..., None], axis=0) + jnp.einsum(
            "ktgs,skd->ktgd",
            tail_w.astype(jnp.bfloat16),
            fresh_val,
            preferred_element_type=jnp.float32,
        )
        attn = (
            (mixed / denom[..., None]).transpose(1, 0, 2, 3).reshape(STEPS, QH * HD).astype(jnp.bfloat16)
        )

    with jax.named_scope("attention_output"):
        h = (
            x.astype(jnp.float32) + jnp.dot(attn, w_out, preferred_element_type=jnp.float32)
        ).astype(jnp.bfloat16)
        u = normalize(h, moe_gain)

    with jax.named_scope("route"):
        row_ids = jnp.arange(routes.shape[0], dtype=jnp.int32)
        picks = jnp.sum(jnp.where((row_ids == device)[:, None, None], routes, 0), axis=0)
        experts = jnp.arange(E, dtype=jnp.int32)
        onehot = (picks[:, :, None] == experts[None, None, :]).astype(jnp.float32)
        logits = jnp.dot(u, router, preferred_element_type=jnp.float32)
        chosen = jnp.sum(onehot * logits[:, None, :], axis=-1)
        share = jax.nn.softmax(chosen, axis=-1)
        weight_te = jnp.sum(share[:, :, None] * onehot, axis=1)
        named = jnp.any(picks[:, :, None] == experts[None, None, :], axis=1)
        rank = jnp.cumsum(named.astype(jnp.int32), axis=0) - 1
        slots = jnp.arange(MOST, dtype=jnp.int32)
        select = (named[:, :, None] & (rank[:, :, None] == slots[None, None, :])).astype(jnp.float32)
        dispatch = jnp.einsum(
            "tej,tm->ejm", select.astype(jnp.bfloat16), u, preferred_element_type=jnp.float32
        ).astype(jnp.bfloat16)
        per_device = devices // E
        sent_u = jnp.broadcast_to(
            dispatch[:, None], (E, per_device, MOST, D)
        ).reshape(devices, MOST, D)

    with jax.named_scope("token_dispatch"):
        arrived = lax.all_to_all(sent_u, ("req", "seq"), 0, 0, tiled=True)

    with jax.named_scope("expert_quarter"):
        hidden = (
            jax.nn.relu(jnp.einsum("sjm,mf->sjf", arrived, w_gate, preferred_element_type=jnp.float32))
            * jnp.einsum("sjm,mf->sjf", arrived, w_up, preferred_element_type=jnp.float32)
        ).astype(jnp.bfloat16)
        produced = jnp.einsum(
            "sjf,fm->sjm", hidden, w_down, preferred_element_type=jnp.float32
        ).astype(jnp.bfloat16)

    with jax.named_scope("expert_return"):
        returned = lax.all_to_all(produced, ("req", "seq"), 0, 0, tiled=True)

    with jax.named_scope("expert_sum"):
        by_expert = jnp.sum(returned.astype(jnp.float32).reshape(E, per_device, MOST, D), axis=1)
        mix = (weight_te[:, :, None] * select).reshape(STEPS, E * MOST)
        moe = jnp.dot(
            mix, by_expert.reshape(E * MOST, D), precision=lax.Precision.HIGHEST,
            preferred_element_type=jnp.float32,
        )
        out = (h.astype(jnp.float32) + moe).astype(jnp.bfloat16)
    return out[:, None, :]


def solution(mesh):
    in_specs = (
        P(None, ("req", "seq"), None),
        P("req"),
        P("req", "seq", None),
        P("req", "seq", None),
        P(),
        P(),
        P(),
        P(),
        P(),
        P(),
        P(None, ("req", "seq")),
        P(None, ("req", "seq")),
        P(("req", "seq"), None),
        P(),
    )
    out_specs = P(None, ("req", "seq"), None)
    return jax.shard_map(
        on_device, mesh=mesh, in_specs=in_specs, out_specs=out_specs, check_vma=False
    )
```

```python
import jax
import jax.numpy as jnp
from jax import lax
from jax.sharding import PartitionSpec as P

D = 1536
QH = 12
KVH = 2
HD = 128
E = 32
EFF = 768
TOP = 4
STEPS = 4
MOST = 2


def normalize(x, gain):
    xf = x.astype(jnp.float32)
    inv = lax.rsqrt(jnp.mean(xf * xf, axis=-1, keepdims=True) + 1e-05)
    return (xf * inv * gain.astype(jnp.float32)).astype(jnp.bfloat16)


def rotate(x, place):
    half = x.shape[-1] // 2
    index = jnp.arange(half, dtype=jnp.float32)
    inverse = jnp.exp(-jnp.log(1000000.0) * 2.0 * index / x.shape[-1])
    angle = place.astype(jnp.float32)[..., None, None] * inverse
    first = x[..., :half]
    second = x[..., half:]
    cosine = jnp.cos(angle)
    sine = jnp.sin(angle)
    return jnp.concatenate(
        [first * cosine - second * sine, second * cosine + first * sine], axis=-1
    )


def on_device(
    tokens,
    lengths,
    k_cache,
    v_cache,
    attn_gain,
    w_qkv,
    sink,
    w_out,
    moe_gain,
    router,
    w_gate,
    w_up,
    w_down,
    routes,
):
    seq_count = lax.axis_size("seq")
    seq_place = lax.axis_index("seq")
    devices = lax.axis_size(("req", "seq"))
    device = lax.axis_index("req") * seq_count + seq_place
    group_rows = lengths.shape[0]
    local_pos = k_cache.shape[1]
    window = local_pos * seq_count
    heads_per = QH // KVH
    scale = HD ** (-0.5)
    step_ids = jnp.arange(STEPS, dtype=jnp.int32)

    x = tokens[:, 0, :]
    own_len = jnp.sum(jnp.where(jnp.arange(group_rows) == seq_place, lengths, 0))
    with jax.named_scope("qkv_projection"):
        a = normalize(x, attn_gain)
        proj = jnp.dot(a, w_qkv, preferred_element_type=jnp.float32)
        place = own_len + step_ids
        query = rotate(proj[:, : QH * HD].reshape(STEPS, QH, HD), place).astype(jnp.bfloat16)
    with jax.named_scope("fresh_key_value"):
        fresh_key = rotate(
            proj[:, QH * HD : (QH + KVH) * HD].reshape(STEPS, KVH, HD), place
        ).astype(jnp.bfloat16)
        fresh_val = proj[:, (QH + KVH) * HD :].reshape(STEPS, KVH, HD).astype(jnp.bfloat16)

    per_head = STEPS * heads_per
    rows_q = KVH * per_head
    q_heads = query.reshape(STEPS, KVH, heads_per, HD).transpose(1, 0, 2, 3)
    with jax.named_scope("query_exchange"):
        sent_q = jnp.broadcast_to(q_heads.reshape(1, rows_q, HD), (seq_count, rows_q, HD))
        every_query = lax.all_to_all(sent_q, "seq", 0, 0, tiled=True)

    with jax.named_scope("slot_attention"):
        key_slot = seq_place * local_pos + jnp.arange(local_pos, dtype=jnp.int32)
        back = jnp.mod(lengths[:, None] - 1 - key_slot[None, :], window)
        row_ids = jnp.arange(rows_q, dtype=jnp.int32)
        row_head = row_ids // per_head
        row_step = (row_ids % per_head) // heads_per
        reach = jnp.minimum(lengths[:, None], window - 1 - row_step[None, :])
        valid = back[:, None, :] < reach[:, :, None]
        lane_head = jnp.arange(KVH * HD, dtype=jnp.int32) // HD
        own_half = row_head[None, :, None] == lane_head[None, None, :]
        q_spread = jnp.where(
            own_half, jnp.concatenate([every_query] * KVH, axis=-1), jnp.zeros((), jnp.bfloat16)
        )
        scores = (
            jnp.einsum("nre,nce->nrc", q_spread, k_cache, preferred_element_type=jnp.float32)
            * scale
        )
        peak = jnp.max(jnp.where(valid, scores, -1e30), axis=-1)
        hi = peak.astype(jnp.bfloat16)
        mid = (peak - hi.astype(jnp.float32)).astype(jnp.bfloat16)
        shard_peak = hi.astype(jnp.float32) + mid.astype(jnp.float32)
        weights = jnp.where(valid, jnp.exp(scores - shard_peak[..., None]), 0.0)
        total_heads = [jnp.sum(weights, axis=-1)]
        hi_heads, mid_heads = [hi], [mid]
        mixed_heads = []
        for k in range(KVH):
            vals_k = v_cache[:, :, k * HD : (k + 1) * HD]
            mixed_heads.append(
                jnp.einsum(
                    "nrc,ncd->nrd",
                    weights[:, k * per_head : (k + 1) * per_head].astype(jnp.bfloat16),
                    vals_k,
                    preferred_element_type=jnp.float32,
                )
            )
        stats = jnp.stack(
            [
                jnp.concatenate(total_heads, axis=1),
                jnp.concatenate(hi_heads, axis=1).astype(jnp.float32),
                jnp.concatenate(mid_heads, axis=1).astype(jnp.float32),
            ],
            axis=1,
        )
        stats = jnp.pad(stats, ((0, 0), (0, 8 - 3), (0, HD - rows_q)))
        packed = jnp.concatenate(mixed_heads + [stats], axis=1).astype(jnp.bfloat16)

    with jax.named_scope("partial_exchange"):
        parts = lax.all_to_all(packed, "seq", 0, 0, tiled=True)

    with jax.named_scope("merge_attention"):
        mixed_s = parts[:, :rows_q, :].astype(jnp.float32).reshape(
            seq_count, KVH, STEPS, heads_per, HD
        )
        total_s = parts[:, rows_q, :rows_q].astype(jnp.float32).reshape(
            seq_count, KVH, STEPS, heads_per
        )
        peak_s = (
            parts[:, rows_q + 1, :rows_q].astype(jnp.float32)
            + parts[:, rows_q + 2, :rows_q].astype(jnp.float32)
        ).reshape(seq_count, KVH, STEPS, heads_per)
        tail_scores = (
            jnp.einsum("ktgd,skd->ktgs", q_heads, fresh_key, preferred_element_type=jnp.float32)
            * scale
        )
        tail_valid = (step_ids[None, :] <= step_ids[:, None])[None, :, None, :]
        sink_grid = sink.reshape(KVH, 1, heads_per)
        final = jnp.maximum(
            jnp.maximum(jnp.max(peak_s, axis=0), jnp.max(jnp.where(tail_valid, tail_scores, -1e30), axis=-1)),
            sink_grid,
        )
        shift = jnp.exp(peak_s - final[None])
        tail_w = jnp.where(tail_valid, jnp.exp(tail_scores - final[..., None]), 0.0)
        denom = (
            jnp.sum(total_s * shift, axis=0)
            + jnp.sum(tail_w, axis=-1)
            + jnp.exp(sink_grid - final)
        )
        mixed = jnp.sum(mixed_s * shift[..., None], axis=0) + jnp.einsum(
            "ktgs,skd->ktgd",
            tail_w.astype(jnp.bfloat16),
            fresh_val,
            preferred_element_type=jnp.float32,
        )
        attn = (
            (mixed / denom[..., None]).transpose(1, 0, 2, 3).reshape(STEPS, QH * HD).astype(jnp.bfloat16)
        )

    with jax.named_scope("attention_output"):
        h = (
            x.astype(jnp.float32) + jnp.dot(attn, w_out, preferred_element_type=jnp.float32)
        ).astype(jnp.bfloat16)
        u = normalize(h, moe_gain)

    with jax.named_scope("route"):
        row_ids = jnp.arange(routes.shape[0], dtype=jnp.int32)
        picks = jnp.sum(jnp.where((row_ids == device)[:, None, None], routes, 0), axis=0)
        experts = jnp.arange(E, dtype=jnp.int32)
        onehot = (picks[:, :, None] == experts[None, None, :]).astype(jnp.float32)
        logits = jnp.dot(u, router, preferred_element_type=jnp.float32)
        chosen = jnp.sum(onehot * logits[:, None, :], axis=-1)
        share = jax.nn.softmax(chosen, axis=-1)
        weight_te = jnp.sum(share[:, :, None] * onehot, axis=1)
        named = jnp.any(picks[:, :, None] == experts[None, None, :], axis=1)
        rank = jnp.cumsum(named.astype(jnp.int32), axis=0) - 1
        slots = jnp.arange(MOST, dtype=jnp.int32)
        select = (named[:, :, None] & (rank[:, :, None] == slots[None, None, :])).astype(jnp.float32)
        dispatch = jnp.einsum(
            "tej,tm->ejm", select.astype(jnp.bfloat16), u, preferred_element_type=jnp.float32
        ).astype(jnp.bfloat16)
        per_device = devices // E
        sent_u = jnp.broadcast_to(
            dispatch[:, None], (E, per_device, MOST, D)
        ).reshape(devices, MOST, D)

    with jax.named_scope("token_dispatch"):
        arrived = lax.all_to_all(sent_u, ("req", "seq"), 0, 0, tiled=True)

    with jax.named_scope("expert_quarter"):
        units = w_gate.shape[1]
        gate_up = jnp.einsum(
            "sjm,mf->sjf", arrived, jnp.concatenate([w_gate, w_up], axis=1),
            preferred_element_type=jnp.float32,
        )
        hidden = (jax.nn.relu(gate_up[..., :units]) * gate_up[..., units:]).astype(jnp.bfloat16)
        produced = jnp.einsum(
            "sjf,fm->sjm", hidden, w_down, preferred_element_type=jnp.float32
        ).astype(jnp.bfloat16)

    with jax.named_scope("expert_return"):
        returned = lax.all_to_all(produced, ("req", "seq"), 0, 0, tiled=True)

    with jax.named_scope("expert_sum"):
        by_expert = jnp.sum(returned.astype(jnp.float32).reshape(E, per_device, MOST, D), axis=1)
        mix = (weight_te[:, :, None] * select).reshape(STEPS, E * MOST)
        moe = jnp.dot(
            mix, by_expert.reshape(E * MOST, D), precision=lax.Precision.HIGHEST,
            preferred_element_type=jnp.float32,
        )
        out = (h.astype(jnp.float32) + moe).astype(jnp.bfloat16)
    return out[:, None, :]


def solution(mesh):
    in_specs = (
        P(None, ("req", "seq"), None),
        P("req"),
        P("req", "seq", None),
        P("req", "seq", None),
        P(),
        P(),
        P(),
        P(),
        P(),
        P(),
        P(None, ("req", "seq")),
        P(None, ("req", "seq")),
        P(("req", "seq"), None),
        P(),
    )
    out_specs = P(None, ("req", "seq"), None)
    return jax.shard_map(
        on_device, mesh=mesh, in_specs=in_specs, out_specs=out_specs, check_vma=False
    )
```

```python
import jax
import jax.numpy as jnp
from jax import lax
from jax.sharding import PartitionSpec as P

D = 1536
QH = 12
KVH = 2
HD = 128
E = 32
EFF = 768
TOP = 4
STEPS = 4
MOST = 2


def normalize(x, gain):
    xf = x.astype(jnp.float32)
    inv = lax.rsqrt(jnp.mean(xf * xf, axis=-1, keepdims=True) + 1e-05)
    return (xf * inv * gain.astype(jnp.float32)).astype(jnp.bfloat16)


def rotate(x, place):
    half = x.shape[-1] // 2
    index = jnp.arange(half, dtype=jnp.float32)
    inverse = jnp.exp(-jnp.log(1000000.0) * 2.0 * index / x.shape[-1])
    angle = place.astype(jnp.float32)[..., None, None] * inverse
    first = x[..., :half]
    second = x[..., half:]
    cosine = jnp.cos(angle)
    sine = jnp.sin(angle)
    return jnp.concatenate(
        [first * cosine - second * sine, second * cosine + first * sine], axis=-1
    )


def on_device(
    tokens,
    lengths,
    k_cache,
    v_cache,
    attn_gain,
    w_qkv,
    sink,
    w_out,
    moe_gain,
    router,
    w_gate,
    w_up,
    w_down,
    routes,
):
    seq_count = lax.axis_size("seq")
    seq_place = lax.axis_index("seq")
    devices = lax.axis_size(("req", "seq"))
    device = lax.axis_index("req") * seq_count + seq_place
    group_rows = lengths.shape[0]
    local_pos = k_cache.shape[1]
    window = local_pos * seq_count
    heads_per = QH // KVH
    scale = HD ** (-0.5)
    step_ids = jnp.arange(STEPS, dtype=jnp.int32)

    x = tokens[:, 0, :]
    own_len = jnp.sum(jnp.where(jnp.arange(group_rows) == seq_place, lengths, 0))
    with jax.named_scope("qkv_projection"):
        a = normalize(x, attn_gain)
        proj = jnp.dot(a, w_qkv, preferred_element_type=jnp.float32)
        place = own_len + step_ids
        query = rotate(proj[:, : QH * HD].reshape(STEPS, QH, HD), place).astype(jnp.bfloat16)
    with jax.named_scope("fresh_key_value"):
        fresh_key = rotate(
            proj[:, QH * HD : (QH + KVH) * HD].reshape(STEPS, KVH, HD), place
        ).astype(jnp.bfloat16)
        fresh_val = proj[:, (QH + KVH) * HD :].reshape(STEPS, KVH, HD).astype(jnp.bfloat16)

    per_head = STEPS * heads_per
    rows_q = KVH * per_head
    q_heads = query.reshape(STEPS, KVH, heads_per, HD).transpose(1, 0, 2, 3)
    with jax.named_scope("query_exchange"):
        sent_q = jnp.broadcast_to(q_heads.reshape(1, rows_q, HD), (seq_count, rows_q, HD))
        every_query = lax.all_to_all(sent_q, "seq", 0, 0, tiled=True)

    with jax.named_scope("slot_attention"):
        key_slot = seq_place * local_pos + jnp.arange(local_pos, dtype=jnp.int32)
        back = jnp.mod(lengths[:, None] - 1 - key_slot[None, :], window)
        row_ids = jnp.arange(rows_q, dtype=jnp.int32)
        row_head = row_ids // per_head
        row_step = (row_ids % per_head) // heads_per
        reach = jnp.minimum(lengths[:, None], window - 1 - row_step[None, :])
        valid = back[:, None, :] < reach[:, :, None]
        lane_head = jnp.arange(KVH * HD, dtype=jnp.int32) // HD
        own_half = row_head[None, :, None] == lane_head[None, None, :]
        q_spread = jnp.where(
            own_half, jnp.concatenate([every_query] * KVH, axis=-1), jnp.zeros((), jnp.bfloat16)
        )
        scores = (
            jnp.einsum("nre,nce->nrc", q_spread, k_cache, preferred_element_type=jnp.float32)
            * scale
        )
        peak = jnp.max(jnp.where(valid, scores, -1e30), axis=-1)
        hi = peak.astype(jnp.bfloat16)
        mid = (peak - hi.astype(jnp.float32)).astype(jnp.bfloat16)
        shard_peak = hi.astype(jnp.float32) + mid.astype(jnp.float32)
        weights = jnp.where(valid, jnp.exp(scores - shard_peak[..., None]), 0.0)
        total_heads = [jnp.sum(weights, axis=-1)]
        hi_heads, mid_heads = [hi], [mid]
        mixed_heads = []
        for k in range(KVH):
            vals_k = v_cache[:, :, k * HD : (k + 1) * HD]
            mixed_heads.append(
                jnp.einsum(
                    "nrc,ncd->nrd",
                    weights[:, k * per_head : (k + 1) * per_head].astype(jnp.bfloat16),
                    vals_k,
                    preferred_element_type=jnp.float32,
                )
            )
        stats = jnp.stack(
            [
                jnp.concatenate(total_heads, axis=1),
                jnp.concatenate(hi_heads, axis=1).astype(jnp.float32),
                jnp.concatenate(mid_heads, axis=1).astype(jnp.float32),
            ],
            axis=1,
        )
        stats = jnp.pad(stats, ((0, 0), (0, 8 - 3), (0, HD - rows_q)))
        packed = jnp.concatenate(mixed_heads + [stats], axis=1).astype(jnp.bfloat16)

    with jax.named_scope("partial_exchange"):
        parts = lax.all_to_all(packed, "seq", 0, 0, tiled=True)

    with jax.named_scope("merge_attention"):
        mixed_s = parts[:, :rows_q, :].astype(jnp.float32).reshape(
            seq_count, KVH, STEPS, heads_per, HD
        )
        total_s = parts[:, rows_q, :rows_q].astype(jnp.float32).reshape(
            seq_count, KVH, STEPS, heads_per
        )
        peak_s = (
            parts[:, rows_q + 1, :rows_q].astype(jnp.float32)
            + parts[:, rows_q + 2, :rows_q].astype(jnp.float32)
        ).reshape(seq_count, KVH, STEPS, heads_per)
        tail_scores = (
            jnp.einsum("ktgd,skd->ktgs", q_heads, fresh_key, preferred_element_type=jnp.float32)
            * scale
        )
        tail_valid = (step_ids[None, :] <= step_ids[:, None])[None, :, None, :]
        sink_grid = sink.reshape(KVH, 1, heads_per)
        final = jnp.maximum(
            jnp.maximum(jnp.max(peak_s, axis=0), jnp.max(jnp.where(tail_valid, tail_scores, -1e30), axis=-1)),
            sink_grid,
        )
        shift = jnp.exp(peak_s - final[None])
        tail_w = jnp.where(tail_valid, jnp.exp(tail_scores - final[..., None]), 0.0)
        denom = (
            jnp.sum(total_s * shift, axis=0)
            + jnp.sum(tail_w, axis=-1)
            + jnp.exp(sink_grid - final)
        )
        mixed = jnp.sum(mixed_s * shift[..., None], axis=0) + jnp.einsum(
            "ktgs,skd->ktgd",
            tail_w.astype(jnp.bfloat16),
            fresh_val,
            preferred_element_type=jnp.float32,
        )
        attn = (
            (mixed / denom[..., None]).transpose(1, 0, 2, 3).reshape(STEPS, QH * HD).astype(jnp.bfloat16)
        )

    with jax.named_scope("attention_output"):
        h = (
            x.astype(jnp.float32) + jnp.dot(attn, w_out, preferred_element_type=jnp.float32)
        ).astype(jnp.bfloat16)
        u = normalize(h, moe_gain)

    with jax.named_scope("route"):
        row_ids = jnp.arange(routes.shape[0], dtype=jnp.int32)
        picks = jnp.sum(jnp.where((row_ids == device)[:, None, None], routes, 0), axis=0)
        experts = jnp.arange(E, dtype=jnp.int32)
        onehot = (picks[:, :, None] == experts[None, None, :]).astype(jnp.float32)
        logits = jnp.dot(u, router, preferred_element_type=jnp.float32)
        chosen = jnp.sum(onehot * logits[:, None, :], axis=-1)
        share = jax.nn.softmax(chosen, axis=-1)
        weight_te = jnp.sum(share[:, :, None] * onehot, axis=1)
        named = jnp.any(picks[:, :, None] == experts[None, None, :], axis=1)
        rank = jnp.cumsum(named.astype(jnp.int32), axis=0) - 1
        slots = jnp.arange(MOST, dtype=jnp.int32)
        select = (named[:, :, None] & (rank[:, :, None] == slots[None, None, :])).astype(jnp.float32)
        dispatch = jnp.einsum(
            "tej,tm->ejm", select.astype(jnp.bfloat16), u, preferred_element_type=jnp.float32
        ).astype(jnp.bfloat16)
        per_device = devices // E
        sent_u = jnp.broadcast_to(
            dispatch[:, None], (E, per_device, MOST, D)
        ).reshape(devices, MOST, D)

    with jax.named_scope("token_dispatch"):
        arrived = lax.all_to_all(sent_u, ("req", "seq"), 0, 0, tiled=True)

    with jax.named_scope("expert_quarter"):
        units = w_gate.shape[1]
        gate_up = jnp.einsum(
            "sjm,mf->sjf", arrived, jnp.concatenate([w_gate, w_up], axis=1),
            preferred_element_type=jnp.float32,
        )
        hidden = (jax.nn.relu(gate_up[..., :units]) * gate_up[..., units:]).astype(jnp.bfloat16)
        produced = jnp.einsum(
            "sjf,fm->sjm", hidden, w_down, preferred_element_type=jnp.float32
        ).astype(jnp.bfloat16)

    with jax.named_scope("expert_return"):
        returned = lax.all_to_all(produced, ("req", "seq"), 0, 0, tiled=True)

    with jax.named_scope("expert_sum"):
        mix = jnp.broadcast_to(
            (weight_te[:, :, None] * select)[:, :, None, :], (STEPS, E, per_device, MOST)
        ).reshape(STEPS, devices * MOST)
        moe = jnp.dot(
            mix, returned.reshape(devices * MOST, D).astype(jnp.float32),
            precision=lax.Precision.HIGHEST, preferred_element_type=jnp.float32,
        )
        out = (h.astype(jnp.float32) + moe).astype(jnp.bfloat16)
    return out[:, None, :]


def solution(mesh):
    in_specs = (
        P(None, ("req", "seq"), None),
        P("req"),
        P("req", "seq", None),
        P("req", "seq", None),
        P(),
        P(),
        P(),
        P(),
        P(),
        P(),
        P(None, ("req", "seq")),
        P(None, ("req", "seq")),
        P(("req", "seq"), None),
        P(),
    )
    out_specs = P(None, ("req", "seq"), None)
    return jax.shard_map(
        on_device, mesh=mesh, in_specs=in_specs, out_specs=out_specs, check_vma=False
    )
```

```python
import jax
import jax.numpy as jnp
from jax import lax
from jax.sharding import PartitionSpec as P

D = 1536
QH = 12
KVH = 2
HD = 128
E = 32
EFF = 768
TOP = 4
STEPS = 4
MOST = 2


def normalize(x, gain):
    xf = x.astype(jnp.float32)
    inv = lax.rsqrt(jnp.mean(xf * xf, axis=-1, keepdims=True) + 1e-05)
    return (xf * inv * gain.astype(jnp.float32)).astype(jnp.bfloat16)


def rotate(x, place):
    half = x.shape[-1] // 2
    index = jnp.arange(half, dtype=jnp.float32)
    inverse = jnp.exp(-jnp.log(1000000.0) * 2.0 * index / x.shape[-1])
    angle = place.astype(jnp.float32)[..., None, None] * inverse
    first = x[..., :half]
    second = x[..., half:]
    cosine = jnp.cos(angle)
    sine = jnp.sin(angle)
    return jnp.concatenate(
        [first * cosine - second * sine, second * cosine + first * sine], axis=-1
    )


def on_device(
    tokens,
    lengths,
    k_cache,
    v_cache,
    attn_gain,
    w_qkv,
    sink,
    w_out,
    moe_gain,
    router,
    w_gate,
    w_up,
    w_down,
    routes,
):
    seq_count = lax.axis_size("seq")
    seq_place = lax.axis_index("seq")
    devices = lax.axis_size(("req", "seq"))
    device = lax.axis_index("req") * seq_count + seq_place
    group_rows = lengths.shape[0]
    local_pos = k_cache.shape[1]
    window = local_pos * seq_count
    heads_per = QH // KVH
    scale = HD ** (-0.5)
    step_ids = jnp.arange(STEPS, dtype=jnp.int32)

    x = tokens[:, 0, :]
    own_len = jnp.sum(jnp.where(jnp.arange(group_rows) == seq_place, lengths, 0))
    with jax.named_scope("qkv_projection"):
        a = normalize(x, attn_gain)
        proj = jnp.dot(a, w_qkv, preferred_element_type=jnp.float32)
        place = own_len + step_ids
        query = rotate(proj[:, : QH * HD].reshape(STEPS, QH, HD), place).astype(jnp.bfloat16)
    with jax.named_scope("fresh_key_value"):
        fresh_key = rotate(
            proj[:, QH * HD : (QH + KVH) * HD].reshape(STEPS, KVH, HD), place
        ).astype(jnp.bfloat16)
        fresh_val = proj[:, (QH + KVH) * HD :].reshape(STEPS, KVH, HD).astype(jnp.bfloat16)

    per_head = STEPS * heads_per
    rows_q = KVH * per_head
    q_heads = query.reshape(STEPS, KVH, heads_per, HD).transpose(1, 0, 2, 3)
    with jax.named_scope("query_exchange"):
        sent_q = jnp.broadcast_to(q_heads.reshape(1, rows_q, HD), (seq_count, rows_q, HD))
        every_query = lax.all_to_all(sent_q, "seq", 0, 0, tiled=True)

    with jax.named_scope("slot_attention"):
        key_slot = seq_place * local_pos + jnp.arange(local_pos, dtype=jnp.int32)
        back = jnp.mod(lengths[:, None] - 1 - key_slot[None, :], window)
        row_ids = jnp.arange(rows_q, dtype=jnp.int32)
        row_head = row_ids // per_head
        row_step = (row_ids % per_head) // heads_per
        reach = jnp.minimum(lengths[:, None], window - 1 - row_step[None, :])
        valid = back[:, None, :] < reach[:, :, None]
        lane_head = jnp.arange(KVH * HD, dtype=jnp.int32) // HD
        own_half = row_head[None, :, None] == lane_head[None, None, :]
        q_spread = jnp.where(
            own_half, jnp.concatenate([every_query] * KVH, axis=-1), jnp.zeros((), jnp.bfloat16)
        )
        scores = (
            jnp.einsum("nre,nce->nrc", q_spread, k_cache, preferred_element_type=jnp.float32)
            * scale
        )
        peak = jnp.max(jnp.where(valid, scores, -1e30), axis=-1)
        hi = peak.astype(jnp.bfloat16)
        mid = (peak - hi.astype(jnp.float32)).astype(jnp.bfloat16)
        shard_peak = hi.astype(jnp.float32) + mid.astype(jnp.float32)
        weights = jnp.where(valid, jnp.exp(scores - shard_peak[..., None]), 0.0)
        total_heads = [jnp.sum(weights, axis=-1)]
        hi_heads, mid_heads = [hi], [mid]
        mixed_heads = []
        for k in range(KVH):
            vals_k = v_cache[:, :, k * HD : (k + 1) * HD]
            mixed_heads.append(
                jnp.einsum(
                    "nrc,ncd->nrd",
                    weights[:, k * per_head : (k + 1) * per_head].astype(jnp.bfloat16),
                    vals_k,
                    preferred_element_type=jnp.float32,
                )
            )
        stats = jnp.stack(
            [
                jnp.concatenate(total_heads, axis=1),
                jnp.concatenate(hi_heads, axis=1).astype(jnp.float32),
                jnp.concatenate(mid_heads, axis=1).astype(jnp.float32),
            ],
            axis=1,
        )
        stats = jnp.pad(stats, ((0, 0), (0, 8 - 3), (0, HD - rows_q)))
        packed = jnp.concatenate(mixed_heads + [stats], axis=1).astype(jnp.bfloat16)

    with jax.named_scope("partial_exchange"):
        parts = lax.all_to_all(packed, "seq", 0, 0, tiled=True)

    with jax.named_scope("merge_attention"):
        mixed_s = parts[:, :rows_q, :].astype(jnp.float32).reshape(
            seq_count, KVH, STEPS, heads_per, HD
        )
        total_s = parts[:, rows_q, :rows_q].astype(jnp.float32).reshape(
            seq_count, KVH, STEPS, heads_per
        )
        peak_s = (
            parts[:, rows_q + 1, :rows_q].astype(jnp.float32)
            + parts[:, rows_q + 2, :rows_q].astype(jnp.float32)
        ).reshape(seq_count, KVH, STEPS, heads_per)
        tail_scores = (
            jnp.einsum("ktgd,skd->ktgs", q_heads, fresh_key, preferred_element_type=jnp.float32)
            * scale
        )
        tail_valid = (step_ids[None, :] <= step_ids[:, None])[None, :, None, :]
        sink_grid = sink.reshape(KVH, 1, heads_per)
        final = jnp.maximum(
            jnp.maximum(jnp.max(peak_s, axis=0), jnp.max(jnp.where(tail_valid, tail_scores, -1e30), axis=-1)),
            sink_grid,
        )
        shift = jnp.exp(peak_s - final[None])
        tail_w = jnp.where(tail_valid, jnp.exp(tail_scores - final[..., None]), 0.0)
        denom = (
            jnp.sum(total_s * shift, axis=0)
            + jnp.sum(tail_w, axis=-1)
            + jnp.exp(sink_grid - final)
        )
        mixed = jnp.sum(mixed_s * shift[..., None], axis=0) + jnp.einsum(
            "ktgs,skd->ktgd",
            tail_w.astype(jnp.bfloat16),
            fresh_val,
            preferred_element_type=jnp.float32,
        )
        attn = (
            (mixed / denom[..., None]).transpose(1, 0, 2, 3).reshape(STEPS, QH * HD).astype(jnp.bfloat16)
        )

    with jax.named_scope("attention_output"):
        h = (
            x.astype(jnp.float32) + jnp.dot(attn, w_out, preferred_element_type=jnp.float32)
        ).astype(jnp.bfloat16)
        u = normalize(h, moe_gain)

    with jax.named_scope("route"):
        row_ids = jnp.arange(routes.shape[0], dtype=jnp.int32)
        picks = jnp.sum(jnp.where((row_ids == device)[:, None, None], routes, 0), axis=0)
        experts = jnp.arange(E, dtype=jnp.int32)
        onehot = (picks[:, :, None] == experts[None, None, :]).astype(jnp.float32)
        logits = jnp.dot(u, router, preferred_element_type=jnp.float32)
        chosen = jnp.sum(onehot * logits[:, None, :], axis=-1)
        share = jax.nn.softmax(chosen, axis=-1)
        weight_te = jnp.sum(share[:, :, None] * onehot, axis=1)
        named = jnp.any(picks[:, :, None] == experts[None, None, :], axis=1)
        rank = jnp.cumsum(named.astype(jnp.int32), axis=0) - 1
        slots = jnp.arange(MOST, dtype=jnp.int32)
        select = (named[:, :, None] & (rank[:, :, None] == slots[None, None, :])).astype(jnp.float32)
        dispatch = jnp.einsum(
            "tej,tm->ejm", select.astype(jnp.bfloat16), u, preferred_element_type=jnp.float32
        ).astype(jnp.bfloat16)
        per_device = devices // E
        sent_u = jnp.broadcast_to(
            dispatch[:, None], (E, per_device, MOST, D)
        ).reshape(devices, MOST, D)

    with jax.named_scope("token_dispatch"):
        arrived = lax.all_to_all(sent_u, ("req", "seq"), 0, 0, tiled=True)

    with jax.named_scope("expert_quarter"):
        units = w_gate.shape[1]
        joined = lax.optimization_barrier(jnp.concatenate([w_gate, w_up], axis=1))
        gate_up = jnp.einsum(
            "sjm,mf->sjf", arrived, joined, preferred_element_type=jnp.float32
        )
        hidden = (jax.nn.relu(gate_up[..., :units]) * gate_up[..., units:]).astype(jnp.bfloat16)
        produced = jnp.einsum(
            "sjf,fm->sjm", hidden, w_down, preferred_element_type=jnp.float32
        ).astype(jnp.bfloat16)

    with jax.named_scope("expert_return"):
        returned = lax.all_to_all(produced, ("req", "seq"), 0, 0, tiled=True)

    with jax.named_scope("expert_sum"):
        by_expert = jnp.sum(returned.astype(jnp.float32).reshape(E, per_device, MOST, D), axis=1)
        mix = (weight_te[:, :, None] * select).reshape(STEPS, E * MOST)
        moe = jnp.dot(
            mix, by_expert.reshape(E * MOST, D), precision=lax.Precision.HIGHEST,
            preferred_element_type=jnp.float32,
        )
        out = (h.astype(jnp.float32) + moe).astype(jnp.bfloat16)
    return out[:, None, :]


def solution(mesh):
    in_specs = (
        P(None, ("req", "seq"), None),
        P("req"),
        P("req", "seq", None),
        P("req", "seq", None),
        P(),
        P(),
        P(),
        P(),
        P(),
        P(),
        P(None, ("req", "seq")),
        P(None, ("req", "seq")),
        P(("req", "seq"), None),
        P(),
    )
    out_specs = P(None, ("req", "seq"), None)
    return jax.shard_map(
        on_device, mesh=mesh, in_specs=in_specs, out_specs=out_specs, check_vma=False
    )
```

```python
import jax
import jax.numpy as jnp
from jax import lax
from jax.sharding import PartitionSpec as P

D = 1536
QH = 12
KVH = 2
HD = 128
E = 32
EFF = 768
TOP = 4
STEPS = 4
MOST = 2


def normalize(x, gain):
    xf = x.astype(jnp.float32)
    inv = lax.rsqrt(jnp.mean(xf * xf, axis=-1, keepdims=True) + 1e-05)
    return (xf * inv * gain.astype(jnp.float32)).astype(jnp.bfloat16)


def rotate(x, place):
    half = x.shape[-1] // 2
    index = jnp.arange(half, dtype=jnp.float32)
    inverse = jnp.exp(-jnp.log(1000000.0) * 2.0 * index / x.shape[-1])
    angle = place.astype(jnp.float32)[..., None, None] * inverse
    first = x[..., :half]
    second = x[..., half:]
    cosine = jnp.cos(angle)
    sine = jnp.sin(angle)
    return jnp.concatenate(
        [first * cosine - second * sine, second * cosine + first * sine], axis=-1
    )


def on_device(
    tokens,
    lengths,
    k_cache,
    v_cache,
    attn_gain,
    w_qkv,
    sink,
    w_out,
    moe_gain,
    router,
    w_gate,
    w_up,
    w_down,
    routes,
):
    seq_count = lax.axis_size("seq")
    seq_place = lax.axis_index("seq")
    devices = lax.axis_size(("req", "seq"))
    device = lax.axis_index("req") * seq_count + seq_place
    group_rows = lengths.shape[0]
    local_pos = k_cache.shape[1]
    window = local_pos * seq_count
    heads_per = QH // KVH
    scale = HD ** (-0.5)
    step_ids = jnp.arange(STEPS, dtype=jnp.int32)

    x = tokens[:, 0, :]
    own_len = jnp.sum(jnp.where(jnp.arange(group_rows) == seq_place, lengths, 0))
    with jax.named_scope("qkv_projection"):
        a = normalize(x, attn_gain)
        proj = jnp.dot(a, w_qkv, preferred_element_type=jnp.float32)
        place = own_len + step_ids
        query = rotate(proj[:, : QH * HD].reshape(STEPS, QH, HD), place).astype(jnp.bfloat16)
    with jax.named_scope("fresh_key_value"):
        fresh_key = rotate(
            proj[:, QH * HD : (QH + KVH) * HD].reshape(STEPS, KVH, HD), place
        ).astype(jnp.bfloat16)
        fresh_val = proj[:, (QH + KVH) * HD :].reshape(STEPS, KVH, HD).astype(jnp.bfloat16)

    per_head = STEPS * heads_per
    rows_q = KVH * per_head
    q_heads = query.reshape(STEPS, KVH, heads_per, HD).transpose(1, 0, 2, 3)
    with jax.named_scope("query_exchange"):
        sent_q = jnp.broadcast_to(q_heads.reshape(1, rows_q, HD), (seq_count, rows_q, HD))
        every_query = lax.all_to_all(sent_q, "seq", 0, 0, tiled=True)

    with jax.named_scope("slot_attention"):
        key_slot = seq_place * local_pos + jnp.arange(local_pos, dtype=jnp.int32)
        back = jnp.mod(lengths[:, None] - 1 - key_slot[None, :], window)
        row_ids = jnp.arange(rows_q, dtype=jnp.int32)
        row_head = row_ids // per_head
        row_step = (row_ids % per_head) // heads_per
        reach = jnp.minimum(lengths[:, None], window - 1 - row_step[None, :])
        valid = back[:, None, :] < reach[:, :, None]
        lane_head = jnp.arange(KVH * HD, dtype=jnp.int32) // HD
        own_half = row_head[None, :, None] == lane_head[None, None, :]
        q_spread = jnp.where(
            own_half, jnp.concatenate([every_query] * KVH, axis=-1), jnp.zeros((), jnp.bfloat16)
        )
        scores = (
            jnp.einsum("nre,nce->nrc", q_spread, k_cache, preferred_element_type=jnp.float32)
            * scale
        )
        peak = jnp.max(jnp.where(valid, scores, -1e30), axis=-1)
        hi = peak.astype(jnp.bfloat16)
        mid = (peak - hi.astype(jnp.float32)).astype(jnp.bfloat16)
        shard_peak = hi.astype(jnp.float32) + mid.astype(jnp.float32)
        weights = jnp.where(valid, jnp.exp(scores - shard_peak[..., None]), 0.0)
        total_heads = [jnp.sum(weights, axis=-1)]
        hi_heads, mid_heads = [hi], [mid]
        mixed_heads = []
        for k in range(KVH):
            vals_k = v_cache[:, :, k * HD : (k + 1) * HD]
            mixed_heads.append(
                jnp.einsum(
                    "nrc,ncd->nrd",
                    weights[:, k * per_head : (k + 1) * per_head].astype(jnp.bfloat16),
                    vals_k,
                    preferred_element_type=jnp.float32,
                )
            )
        stats = jnp.stack(
            [
                jnp.concatenate(total_heads, axis=1),
                jnp.concatenate(hi_heads, axis=1).astype(jnp.float32),
                jnp.concatenate(mid_heads, axis=1).astype(jnp.float32),
            ],
            axis=1,
        )
        stats = jnp.pad(stats, ((0, 0), (0, 8 - 3), (0, HD - rows_q)))
        packed = jnp.concatenate(mixed_heads + [stats], axis=1).astype(jnp.bfloat16)

    with jax.named_scope("partial_exchange"):
        parts = lax.all_to_all(packed, "seq", 0, 0, tiled=True)

    with jax.named_scope("merge_attention"):
        mixed_s = parts[:, :rows_q, :].astype(jnp.float32).reshape(
            seq_count, KVH, STEPS, heads_per, HD
        )
        total_s = parts[:, rows_q, :rows_q].astype(jnp.float32).reshape(
            seq_count, KVH, STEPS, heads_per
        )
        peak_s = (
            parts[:, rows_q + 1, :rows_q].astype(jnp.float32)
            + parts[:, rows_q + 2, :rows_q].astype(jnp.float32)
        ).reshape(seq_count, KVH, STEPS, heads_per)
        tail_scores = (
            jnp.einsum("ktgd,skd->ktgs", q_heads, fresh_key, preferred_element_type=jnp.float32)
            * scale
        )
        tail_valid = (step_ids[None, :] <= step_ids[:, None])[None, :, None, :]
        sink_grid = sink.reshape(KVH, 1, heads_per)
        final = jnp.maximum(
            jnp.maximum(jnp.max(peak_s, axis=0), jnp.max(jnp.where(tail_valid, tail_scores, -1e30), axis=-1)),
            sink_grid,
        )
        shift = jnp.exp(peak_s - final[None])
        tail_w = jnp.where(tail_valid, jnp.exp(tail_scores - final[..., None]), 0.0)
        denom = (
            jnp.sum(total_s * shift, axis=0)
            + jnp.sum(tail_w, axis=-1)
            + jnp.exp(sink_grid - final)
        )
        mixed = jnp.sum(mixed_s * shift[..., None], axis=0) + jnp.einsum(
            "ktgs,skd->ktgd",
            tail_w.astype(jnp.bfloat16),
            fresh_val,
            preferred_element_type=jnp.float32,
        )
        attn = (
            (mixed / denom[..., None]).transpose(1, 0, 2, 3).reshape(STEPS, QH * HD).astype(jnp.bfloat16)
        )

    with jax.named_scope("attention_output"):
        h = (
            x.astype(jnp.float32) + jnp.dot(attn, w_out, preferred_element_type=jnp.float32)
        ).astype(jnp.bfloat16)
        u = normalize(h, moe_gain)

    with jax.named_scope("route"):
        row_ids = jnp.arange(routes.shape[0], dtype=jnp.int32)
        picks = jnp.sum(jnp.where((row_ids == device)[:, None, None], routes, 0), axis=0)
        experts = jnp.arange(E, dtype=jnp.int32)
        onehot = (picks[:, :, None] == experts[None, None, :]).astype(jnp.float32)
        logits = jnp.dot(u, router, preferred_element_type=jnp.float32)
        chosen = jnp.sum(onehot * logits[:, None, :], axis=-1)
        share = jax.nn.softmax(chosen, axis=-1)
        weight_te = jnp.sum(share[:, :, None] * onehot, axis=1)
        named = jnp.any(picks[:, :, None] == experts[None, None, :], axis=1)
        rank = jnp.cumsum(named.astype(jnp.int32), axis=0) - 1
        slots = jnp.arange(MOST, dtype=jnp.int32)
        select = (named[:, :, None] & (rank[:, :, None] == slots[None, None, :])).astype(jnp.float32)
        dispatch = jnp.einsum(
            "tej,tm->ejm", select.astype(jnp.bfloat16), u, preferred_element_type=jnp.float32
        ).astype(jnp.bfloat16)
        per_device = devices // E
        sent_u = jnp.broadcast_to(
            dispatch[:, None], (E, per_device, MOST, D)
        ).reshape(devices, MOST, D)

    with jax.named_scope("token_dispatch"):
        arrived = lax.all_to_all(sent_u, ("req", "seq"), 0, 0, tiled=True)

    with jax.named_scope("expert_quarter"):
        units = w_gate.shape[1]
        gate_up = jnp.dot(
            arrived.reshape(devices * MOST, D), jnp.concatenate([w_gate, w_up], axis=1),
            preferred_element_type=jnp.float32,
        )
        hidden = (jax.nn.relu(gate_up[..., :units]) * gate_up[..., units:]).astype(jnp.bfloat16)
        produced = (
            jnp.dot(hidden, w_down, preferred_element_type=jnp.float32)
            .astype(jnp.bfloat16)
            .reshape(devices, MOST, D)
        )

    with jax.named_scope("expert_return"):
        returned = lax.all_to_all(produced, ("req", "seq"), 0, 0, tiled=True)

    with jax.named_scope("expert_sum"):
        by_expert = jnp.sum(returned.astype(jnp.float32).reshape(E, per_device, MOST, D), axis=1)
        mix = (weight_te[:, :, None] * select).reshape(STEPS, E * MOST)
        moe = jnp.dot(
            mix, by_expert.reshape(E * MOST, D), precision=lax.Precision.HIGHEST,
            preferred_element_type=jnp.float32,
        )
        out = (h.astype(jnp.float32) + moe).astype(jnp.bfloat16)
    return out[:, None, :]


def solution(mesh):
    in_specs = (
        P(None, ("req", "seq"), None),
        P("req"),
        P("req", "seq", None),
        P("req", "seq", None),
        P(),
        P(),
        P(),
        P(),
        P(),
        P(),
        P(None, ("req", "seq")),
        P(None, ("req", "seq")),
        P(("req", "seq"), None),
        P(),
    )
    out_specs = P(None, ("req", "seq"), None)
    return jax.shard_map(
        on_device, mesh=mesh, in_specs=in_specs, out_specs=out_specs, check_vma=False
    )
```
